512 devices in a mesh: line: 32 (over z_lo, x, core), seg: 16 (over z_hi, y).
Axes of the slice: x: 4, y: 4, z: 16 (z_hi: 4, z_lo: 4; z = z_hi * 4 + z_lo), core: 2. Of those that a mesh axis runs over, the one named last changes fastest.
Arguments:
- right_side: float32 [32, 128, 96, 128], P('line', 'seg'), may hold values from -24 to 24
- band_blocks: bfloat16 [32, 128, 4, 96, 96], P('line', 'seg')
- knot_pairs: int32 [32, 16, 6, 2, 2], P('line', 'seg'), may hold values from 0 to 7
- pair_counts: int32 [32, 16, 6], P('line', 'seg'), may hold values from 1 to 2, as said below
- cross_blocks: bfloat16 [32, 16, 6, 2, 96, 96], P('line', 'seg'), may hold values from -0.359375 to 0.359375
Outputs:
- solution: float32 [32, 128, 96, 128], P('line', 'seg')
The draws below stay inside these ranges and needn't reach their ends.
Inputs may be any that keep to these rules, and one draw needn't show every extreme that they name: `knot_pairs`: entry s of bucket b counts only if s < pair_counts of that bucket; other entries are unused. `pair_counts`: every bucket holds at least one pair, and in every draw some line and segment has all buckets full.
All inputs are finite; a program needn't handle non-finite values.
Results may differ from the reference program's by a relative error of at most 0.0028.
Values may be sent and summed in bfloat16 or wider, within the bound.
No kernel may reach another device: no remote copies, remote signals or barrier semaphores. Data moves between devices by JAX's collectives and lax.ppermute only.
A program may use at most 64 MiB of HBM per device.

```python
import math
import jax
import jax.numpy as jnp
from jax import lax

PARAMS = 96
PROBES = 128
KNOT_DEV = 8
GROUP = 4
CAP = 2
ITERS = 3
LINES = 32
SEGS = 16
KNOTS = 128
BUCKETS = 6


def band_sample(line_key):
    shape = (KNOTS, 4, PARAMS, PARAMS)
    sigma = 0.4 / math.sqrt(PARAMS)
    base = jax.random.normal(line_key, shape, jnp.float32) * sigma
    levels = jnp.exp(jax.random.uniform(jax.random.fold_in(line_key, 7), (KNOTS, PARAMS), jnp.float32, math.log(4.0), math.log(8.0)))
    first = base[:, 0]
    symmetric = (first + jnp.swapaxes(first, -1, -2)) * 0.70710678
    eye_block = jnp.eye(PARAMS, dtype=jnp.float32)
    diag_block = symmetric + levels[:, :, None] * eye_block
    return base.at[:, 0].set(diag_block)


def draw_band_blocks(key, part):
    line_keys = jax.vmap(lambda index: jax.random.fold_in(key, index))(jnp.arange(LINES))
    whole = lax.map(band_sample, line_keys)
    return whole.astype(jnp.bfloat16)


def draw_pair_counts(key, part):
    base = jax.random.randint(key, (LINES, SEGS, BUCKETS), 1, CAP + 1, jnp.int32)
    pick_line = jax.random.randint(jax.random.fold_in(key, 1), (), 0, LINES, jnp.int32)
    pick_seg = jax.random.randint(jax.random.fold_in(key, 2), (), 0, SEGS, jnp.int32)
    chosen = (jnp.arange(LINES, dtype=jnp.int32)[:, None] == pick_line) & (jnp.arange(SEGS, dtype=jnp.int32)[None, :] == pick_seg)
    base = jnp.where(chosen[:, :, None], CAP, base)
    return base.astype(jnp.int32)


def set_ends(entries, own_key, low, high):
    spot = [jax.random.randint(jax.random.fold_in(own_key, axis), (), 0, length) for axis, length in enumerate(entries.shape)]
    widest = entries.shape.index(max(entries.shape))
    neighbour = spot[:widest] + [(spot[widest] + 1) % entries.shape[widest]] + spot[widest + 1:]
    return entries.at[tuple(spot)].set(low).at[tuple(neighbour)].set(high)


def block_scale(stream_key, extent, pieces, least, top_value):
    def one(position, parts):
        draws = jax.random.uniform(jax.random.fold_in(jax.random.fold_in(stream_key, 6), position), (parts,), jnp.float32, least / len(pieces), top_value / len(pieces))
        return jnp.repeat(jnp.exp(draws), extent[position] // parts).reshape((-1,) + (1,) * (len(extent) - position - 1))

    gain = one(*pieces[0])
    for cut in pieces[1:]:
        gain = gain * one(*cut)
    return gain


def gaussian(own_key, shape, spread, bound, cuts=(), held_as=jnp.bfloat16):
    loudness = block_scale(own_key, shape, cuts, -0.22, 0.18) if cuts else 1.0
    entries = jax.random.normal(own_key, shape, jnp.float32) * spread * loudness
    return jnp.minimum(jnp.maximum(entries, -bound), bound).astype(held_as)


def setup_inputs(seed: int = 0) -> dict:
    splits = jax.random.split(jax.random.key(seed), 6)
    right_side = gaussian(splits[0], (LINES, KNOTS, PARAMS, PROBES), 4.0, 24.0, ((0, 32), (1, 16)), jnp.float32)
    band_blocks = draw_band_blocks(jax.random.fold_in(splits[5], 71), 0)
    knot_pairs = set_ends(jax.random.randint(splits[2], (LINES, SEGS, BUCKETS, CAP, 2), 0, KNOT_DEV), jax.random.fold_in(splits[2], 1), 0, KNOT_DEV - 1).astype(jnp.int32)
    pair_counts = draw_pair_counts(jax.random.fold_in(splits[5], 71), 0)
    cross_blocks = gaussian(splits[4], (LINES, SEGS, BUCKETS, CAP, PARAMS, PARAMS), 0.06, 0.359375, ((0, 32), (1, 16)))
    return dict(right_side=right_side, band_blocks=band_blocks, knot_pairs=knot_pairs, pair_counts=pair_counts, cross_blocks=cross_blocks)


LO_BOUND = 1.5
HI_BOUND = 12.0


def bucket_offsets():
    return [b - (GROUP - 1) if b < GROUP - 1 else b - GROUP + 2 for b in range(BUCKETS)]


def band_apply(line_blocks, search_vector):
    blocks = line_blocks.astype(jnp.float32)
    padded = jnp.pad(search_vector, ((3, 3), (0, 0), (0, 0)))
    summed = jnp.zeros(search_vector.shape, jnp.float32)
    for step in range(4):
        summed = summed + jnp.einsum('kab,kbr->kar', blocks[:, step], padded[3 + step:3 + step + KNOTS], precision=lax.Precision.HIGHEST)
    for step in range(1, 4):
        lower_term = jnp.einsum('kba,kbr->kar', blocks[:KNOTS - step, step], search_vector[:KNOTS - step], precision=lax.Precision.HIGHEST)
        summed = summed + jnp.pad(lower_term, ((step, 0), (0, 0), (0, 0)))
    return summed


def operator(probe_bf, band_blocks, knot_pairs, pair_counts, cross_blocks):
    search_vector = probe_bf.astype(jnp.float32)
    iterate_output = lax.map(lambda pair: band_apply(pair[0], pair[1]), (band_blocks, search_vector))
    offsets = bucket_offsets()
    line_ids = jnp.arange(LINES).astype(jnp.int32)[:, None, None]
    seg_ids = jnp.arange(SEGS).astype(jnp.int32)[None, :, None]
    slot_ids = jnp.arange(CAP).astype(jnp.int32)[None, None, :]
    zeros_idx = jnp.zeros((LINES, SEGS, CAP), jnp.int32)
    for bucket in range(BUCKETS):
        occupied_mask = slot_ids < pair_counts[:, :, bucket][..., None]
        home_knot = (seg_ids * KNOT_DEV + knot_pairs[:, :, bucket, :, 0]).astype(jnp.int32)
        far_knot = (seg_ids * KNOT_DEV + knot_pairs[:, :, bucket, :, 1]).astype(jnp.int32)
        home_line = (line_ids + zeros_idx).astype(jnp.int32)
        far_line = ((line_ids + offsets[bucket] + LINES) % LINES).astype(jnp.int32) + zeros_idx
        weight = occupied_mask.astype(jnp.float32)[..., None, None]
        blocks = cross_blocks[:, :, bucket].astype(jnp.float32)
        far_vec = search_vector[far_line, far_knot]
        home_vec = search_vector[home_line, home_knot]
        forward = jnp.einsum('lscab,lscbr->lscar', blocks, far_vec, precision=lax.Precision.HIGHEST) * weight
        backward = jnp.einsum('lscba,lscbr->lscar', blocks, home_vec, precision=lax.Precision.HIGHEST) * weight
        iterate_output = iterate_output.at[home_line, home_knot].add(forward)
        iterate_output = iterate_output.at[far_line, far_knot].add(backward)
    return iterate_output


def reference(right_side, band_blocks, knot_pairs, pair_counts, cross_blocks):
    center = (HI_BOUND + LO_BOUND) / 2.0
    radius = (HI_BOUND - LO_BOUND) / 2.0
    coeff = radius / center
    solution = jnp.zeros(right_side.shape, jnp.float32)
    residual = right_side
    direction = right_side / center
    for turn in range(ITERS):
        probe_bf = direction.astype(jnp.bfloat16)
        solution = solution + direction
        residual = residual - operator(probe_bf, band_blocks, knot_pairs, pair_counts, cross_blocks)
        coeff_next = 1.0 / (2.0 * center / radius - coeff)
        direction = (coeff_next * coeff) * direction + (2.0 * coeff_next / radius) * residual
        coeff = coeff_next
    return solution + direction
```

```python
import jax
import jax.numpy as jnp
from jax import lax
from jax.sharding import PartitionSpec as P

ITERS = 3


LO_BOUND = 1.5
HI_BOUND = 12.0


def shifted_open(value, axis, steps):
    count = lax.axis_size(axis)
    initial, last = (max(0, -steps), min(count, count - steps))
    return lax.ppermute(value, axis, [(source, source + steps) for source in range(initial, last)])


def shifted_ring(value, axis, steps):
    count = lax.axis_size(axis)
    return lax.ppermute(value, axis, [(i, (i + steps) % count) for i in range(count)])


def body(right_side, band_blocks, knot_pairs, pair_counts, cross_blocks):
    right_rows = right_side[0]
    blocks = band_blocks[0]
    my_pairs = knot_pairs[0, 0]
    used_count = pair_counts[0, 0]
    couplings = cross_blocks[0, 0]
    knots, params, probes = right_rows.shape
    buckets, slots = my_pairs.shape[0], my_pairs.shape[1]
    group_span = buckets // 2 + 1
    offsets = [
        b - (group_span - 1) if b < group_span - 1 else b - group_span + 2 for b in range(buckets)
    ]
    bucket_of = {o: b for b, o in enumerate(offsets)}
    shifts = [o for o in offsets if o > 0] + [o for o in offsets if o < 0]
    lines = lax.axis_size("line")
    me = lax.axis_index("line")

    boundary_blocks = shifted_open(blocks[knots - 3 :], "seg", 1)
    lower_blocks = jnp.concatenate([boundary_blocks, blocks], axis=0)

    used = jnp.arange(slots, dtype=jnp.int32)[None, :] < used_count[:, None]
    own_knot = jnp.where(used, my_pairs[:, :, 0], -1)
    far_knot = jnp.where(used, my_pairs[:, :, 1], -1)
    table = lax.all_gather(far_knot, "line")

    answer_knots = []
    landing_knots = []
    for s in shifts:
        answer_knots.append(lax.dynamic_index_in_dim(table, (me + s) % lines, 0, False)[bucket_of[-s]])
        landing_knots.append(lax.dynamic_index_in_dim(table, (me - s + lines) % lines, 0, False)[bucket_of[s]])
    knot_ids = jnp.arange(knots, dtype=jnp.int32)
    pick_index = jnp.concatenate([own_knot.reshape(-1)] + answer_knots)
    pick = (pick_index[:, None] == knot_ids[None, :]).astype(jnp.bfloat16)
    own_place = (own_knot.reshape(-1)[None, :] == knot_ids[:, None]).astype(jnp.float32)
    land_place = (jnp.concatenate(landing_knots)[None, :] == knot_ids[:, None]).astype(jnp.bfloat16)

    center = (HI_BOUND + LO_BOUND) / 2.0
    radius = (HI_BOUND - LO_BOUND) / 2.0
    coeff = radius / center
    solution = jnp.zeros(right_rows.shape, jnp.float32)
    residual = right_rows
    direction = right_rows / center
    own_rows = buckets * slots
    for turn in range(ITERS):
        probe_bf = direction.astype(jnp.bfloat16)
        solution = solution + direction
        picked = jnp.einsum(
            "sk,kpr->spr", pick, probe_bf, preferred_element_type=jnp.float32
        ).astype(jnp.bfloat16)
        resident = picked[:own_rows].reshape(buckets, slots, params, probes)
        answers = picked[own_rows:].reshape(len(shifts), slots, params, probes)
        product = jnp.einsum(
            "bsqp,bsqr->bspr", couplings, resident, preferred_element_type=jnp.float32
        ).astype(jnp.bfloat16)
        fetched = [None] * buckets
        landed = []
        for t, s in enumerate(shifts):
            message = jnp.concatenate([answers[t], product[bucket_of[s]]], axis=0)
            got = shifted_ring(message, "line", s)
            fetched[bucket_of[-s]] = got[:slots]
            landed.append(got[slots:])
        low = shifted_open(probe_bf[knots - 3 :], "seg", 1)
        high = shifted_open(probe_bf[:3], "seg", -1)
        extended = jnp.concatenate([low, probe_bf, high], axis=0)
        summed = jnp.zeros(probe_bf.shape, jnp.float32)
        for step in range(4):
            summed = summed + jnp.einsum(
                "kab,kbr->kar",
                blocks[:, step],
                extended[3 + step : 3 + step + knots],
                preferred_element_type=jnp.float32,
            )
        for step in range(1, 4):
            summed = summed + jnp.einsum(
                "kba,kbr->kar",
                lower_blocks[3 - step : 3 - step + knots, step],
                extended[3 - step : 3 - step + knots],
                preferred_element_type=jnp.float32,
            )
        fetched = jnp.stack(fetched)
        forward = jnp.einsum(
            "bsqp,bspr->bsqr", couplings, fetched, preferred_element_type=jnp.float32
        ).reshape(own_rows, params, probes)
        landed = jnp.concatenate(landed, axis=0)
        cross = jnp.einsum(
            "ks,spr->kpr", own_place, forward, precision=lax.Precision.HIGHEST
        ) + jnp.einsum("ks,spr->kpr", land_place, landed, preferred_element_type=jnp.float32)
        residual = residual - (summed + cross)
        coeff_next = 1.0 / (2.0 * center / radius - coeff)
        direction = coeff_next * coeff * direction + 2.0 * coeff_next / radius * residual
        coeff = coeff_next
    return (solution + direction)[None]


def solution(mesh):
    return jax.shard_map(
        body,
        mesh=mesh,
        in_specs=(
            P("line", "seg", None, None),
            P("line", "seg", None, None, None),
            P("line", "seg", None, None, None),
            P("line", "seg", None),
            P("line", "seg", None, None, None, None),
        ),
        out_specs=P("line", "seg", None, None),
        check_vma=False,
    )
```

```python
import jax
import jax.numpy as jnp
from jax import lax
from jax.sharding import PartitionSpec as P

ITERS = 3


LO_BOUND = 1.5
HI_BOUND = 12.0


def shifted_open(value, axis, steps):
    count = lax.axis_size(axis)
    initial, last = (max(0, -steps), min(count, count - steps))
    return lax.ppermute(value, axis, [(source, source + steps) for source in range(initial, last)])


def shifted_ring(value, axis, steps):
    count = lax.axis_size(axis)
    return lax.ppermute(value, axis, [(i, (i + steps) % count) for i in range(count)])


def body(right_side, band_blocks, knot_pairs, pair_counts, cross_blocks):
    right_rows = right_side[0]
    blocks = band_blocks[0]
    my_pairs = knot_pairs[0, 0]
    used_count = pair_counts[0, 0]
    couplings = cross_blocks[0, 0]
    knots, params, probes = right_rows.shape
    buckets, slots = my_pairs.shape[0], my_pairs.shape[1]
    group_span = buckets // 2 + 1
    offsets = [
        b - (group_span - 1) if b < group_span - 1 else b - group_span + 2 for b in range(buckets)
    ]
    bucket_of = {o: b for b, o in enumerate(offsets)}
    shifts = [o for o in offsets if o > 0] + [o for o in offsets if o < 0]

    boundary_blocks = shifted_open(blocks[knots - 3 :], "seg", 1)
    lower_blocks = jnp.concatenate([boundary_blocks, blocks], axis=0)

    used = jnp.arange(slots, dtype=jnp.int32)[None, :] < used_count[:, None]
    own_knot = jnp.where(used, my_pairs[:, :, 0], -1)
    far_knot = jnp.where(used, my_pairs[:, :, 1], -1)
    knot_ids = jnp.arange(knots, dtype=jnp.int32)
    own_pick = (own_knot.reshape(-1)[:, None] == knot_ids[None, :]).astype(jnp.bfloat16)
    own_place = (own_knot.reshape(-1)[None, :] == knot_ids[:, None]).astype(jnp.float32)
    far_pick = (far_knot[:, :, None] == knot_ids[None, None, :]).astype(jnp.bfloat16)
    index_rows = jnp.zeros((buckets, 1, params, probes), jnp.bfloat16)
    index_rows = index_rows.at[:, 0, 0, :slots].set(far_knot.astype(jnp.bfloat16))
    knot_vals = knot_ids.astype(jnp.float32)
    answer_pick = None
    land_place = None

    center = (HI_BOUND + LO_BOUND) / 2.0
    radius = (HI_BOUND - LO_BOUND) / 2.0
    coeff = radius / center
    solution = jnp.zeros(right_rows.shape, jnp.float32)
    residual = right_rows
    direction = right_rows / center
    own_rows = buckets * slots
    for turn in range(ITERS):
        probe_bf = direction.astype(jnp.bfloat16)
        solution = solution + direction
        if answer_pick is None:
            picked = jnp.einsum(
                "sk,kpr->spr", own_pick, probe_bf, preferred_element_type=jnp.float32
            ).astype(jnp.bfloat16)
            resident = picked.reshape(buckets, slots, params, probes)
        else:
            picked = jnp.einsum(
                "sk,kpr->spr",
                jnp.concatenate([own_pick, answer_pick], axis=0),
                probe_bf,
                preferred_element_type=jnp.float32,
            ).astype(jnp.bfloat16)
            resident = picked[:own_rows].reshape(buckets, slots, params, probes)
            answers = picked[own_rows:].reshape(len(shifts), slots, params, probes)
        product = jnp.einsum(
            "bsqp,bsqr->bspr", couplings, resident, preferred_element_type=jnp.float32
        ).astype(jnp.bfloat16)
        fetched = [None] * buckets
        landed = []
        got_index = {}
        for t, s in enumerate(shifts):
            if answer_pick is None:
                message = jnp.concatenate(
                    [probe_bf, product[bucket_of[s]], index_rows[bucket_of[s]]], axis=0
                )
            else:
                message = jnp.concatenate([answers[t], product[bucket_of[s]]], axis=0)
            got = shifted_ring(message, "line", s)
            if answer_pick is None:
                fetched[bucket_of[-s]] = jnp.einsum(
                    "sk,kpr->spr",
                    far_pick[bucket_of[-s]],
                    got[:knots],
                    preferred_element_type=jnp.float32,
                ).astype(jnp.bfloat16)
                landed.append(got[knots : knots + slots])
                got_index[s] = got[knots + slots, 0, :slots].astype(jnp.float32)
            else:
                fetched[bucket_of[-s]] = got[:slots]
                landed.append(got[slots:])
        if answer_pick is None:
            answer_pick = jnp.concatenate(
                [(got_index[-s][:, None] == knot_vals[None, :]) for s in shifts], axis=0
            ).astype(jnp.bfloat16)
            land_place = jnp.concatenate(
                [(got_index[s][None, :] == knot_vals[:, None]) for s in shifts], axis=1
            ).astype(jnp.bfloat16)
        low = shifted_open(probe_bf[knots - 3 :], "seg", 1)
        high = shifted_open(probe_bf[:3], "seg", -1)
        extended = jnp.concatenate([low, probe_bf, high], axis=0)
        summed = jnp.zeros(probe_bf.shape, jnp.float32)
        for step in range(4):
            summed = summed + jnp.einsum(
                "kab,kbr->kar",
                blocks[:, step],
                extended[3 + step : 3 + step + knots],
                preferred_element_type=jnp.float32,
            )
        for step in range(1, 4):
            summed = summed + jnp.einsum(
                "kba,kbr->kar",
                lower_blocks[3 - step : 3 - step + knots, step],
                extended[3 - step : 3 - step + knots],
                preferred_element_type=jnp.float32,
            )
        fetched = jnp.stack(fetched)
        forward = jnp.einsum(
            "bsqp,bspr->bsqr", couplings, fetched, preferred_element_type=jnp.float32
        ).reshape(own_rows, params, probes)
        landed = jnp.concatenate(landed, axis=0)
        cross = jnp.einsum(
            "ks,spr->kpr", own_place, forward, precision=lax.Precision.HIGHEST
        ) + jnp.einsum("ks,spr->kpr", land_place, landed, preferred_element_type=jnp.float32)
        residual = residual - (summed + cross)
        coeff_next = 1.0 / (2.0 * center / radius - coeff)
        direction = coeff_next * coeff * direction + 2.0 * coeff_next / radius * residual
        coeff = coeff_next
    return (solution + direction)[None]


def solution(mesh):
    return jax.shard_map(
        body,
        mesh=mesh,
        in_specs=(
            P("line", "seg", None, None),
            P("line", "seg", None, None, None),
            P("line", "seg", None, None, None),
            P("line", "seg", None),
            P("line", "seg", None, None, None, None),
        ),
        out_specs=P("line", "seg", None, None),
        check_vma=False,
    )
```

```python
import jax
import jax.numpy as jnp
from jax import lax
from jax.sharding import PartitionSpec as P

ITERS = 3


LO_BOUND = 1.5
HI_BOUND = 12.0


def shifted_open(value, axis, steps):
    count = lax.axis_size(axis)
    initial, last = (max(0, -steps), min(count, count - steps))
    return lax.ppermute(value, axis, [(source, source + steps) for source in range(initial, last)])


def shifted_ring(value, axis, steps):
    count = lax.axis_size(axis)
    return lax.ppermute(value, axis, [(i, (i + steps) % count) for i in range(count)])


def body(right_side, band_blocks, knot_pairs, pair_counts, cross_blocks):
    right_rows = right_side[0]
    blocks = band_blocks[0]
    my_pairs = knot_pairs[0, 0]
    used_count = pair_counts[0, 0]
    couplings = cross_blocks[0, 0]
    knots, params, probes = right_rows.shape
    buckets, slots = my_pairs.shape[0], my_pairs.shape[1]
    group_span = buckets // 2 + 1
    offsets = [
        b - (group_span - 1) if b < group_span - 1 else b - group_span + 2 for b in range(buckets)
    ]
    bucket_of = {o: b for b, o in enumerate(offsets)}
    shifts = [o for o in offsets if o > 0] + [o for o in offsets if o < 0]

    boundary_blocks = shifted_open(blocks[knots - 3 :], "seg", 1)
    lower_blocks = jnp.concatenate([boundary_blocks, blocks], axis=0)

    used = jnp.arange(slots, dtype=jnp.int32)[None, :] < used_count[:, None]
    own_knot = jnp.where(used, my_pairs[:, :, 0], -1)
    far_knot = jnp.where(used, my_pairs[:, :, 1], -1)
    knot_ids = jnp.arange(knots, dtype=jnp.int32)
    own_pick = (own_knot.reshape(-1)[:, None] == knot_ids[None, :]).astype(jnp.bfloat16)
    own_place = (own_knot.reshape(-1)[None, :] == knot_ids[:, None]).astype(jnp.float32)
    far_pick = (far_knot[:, :, None] == knot_ids[None, None, :]).astype(jnp.bfloat16)
    index_rows = jnp.zeros((buckets, 1, params, probes), jnp.bfloat16)
    index_rows = index_rows.at[:, 0, 0, :slots].set(far_knot.astype(jnp.bfloat16))
    knot_vals = knot_ids.astype(jnp.float32)
    ext_knots = knots + 6
    ext_ids = jnp.arange(ext_knots, dtype=jnp.int32)
    band_weight = None
    for step in range(4):
        place = (ext_ids[None, :] == knot_ids[:, None] + 3 + step).astype(jnp.float32)
        term = jnp.einsum("km,kab->kamb", place, blocks[:, step].astype(jnp.float32))
        band_weight = term if band_weight is None else band_weight + term
    for step in range(1, 4):
        place = (ext_ids[None, :] == knot_ids[:, None] + 3 - step).astype(jnp.float32)
        band_weight = band_weight + jnp.einsum(
            "km,kba->kamb", place, lower_blocks[3 - step : 3 - step + knots, step].astype(jnp.float32)
        )
    fetch_order = [bucket_of[-s] for s in shifts]
    fetch_place = jnp.concatenate(
        [own_place.reshape(knots, buckets, slots)[:, b] for b in fetch_order], axis=1
    )
    fetch_blocks = jnp.concatenate([couplings[b] for b in fetch_order], axis=0).astype(jnp.float32)
    fetch_weight = jnp.einsum("kf,fab->kafb", fetch_place, fetch_blocks)
    weight = jnp.concatenate([band_weight, fetch_weight], axis=2).astype(jnp.bfloat16)
    answer_pick = None
    land_place = None

    center = (HI_BOUND + LO_BOUND) / 2.0
    radius = (HI_BOUND - LO_BOUND) / 2.0
    coeff = radius / center
    solution = jnp.zeros(right_rows.shape, jnp.float32)
    residual = right_rows
    direction = right_rows / center
    own_rows = buckets * slots
    for turn in range(ITERS):
        probe_bf = direction.astype(jnp.bfloat16)
        solution = solution + direction
        if answer_pick is None:
            picked = jnp.einsum(
                "sk,kpr->spr", own_pick, probe_bf, preferred_element_type=jnp.float32
            ).astype(jnp.bfloat16)
            resident = picked.reshape(buckets, slots, params, probes)
        else:
            picked = jnp.einsum(
                "sk,kpr->spr",
                jnp.concatenate([own_pick, answer_pick], axis=0),
                probe_bf,
                preferred_element_type=jnp.float32,
            ).astype(jnp.bfloat16)
            resident = picked[:own_rows].reshape(buckets, slots, params, probes)
            answers = picked[own_rows:].reshape(len(shifts), slots, params, probes)
        product = jnp.einsum(
            "bsqp,bsqr->bspr", couplings, resident, preferred_element_type=jnp.float32
        ).astype(jnp.bfloat16)
        fetched = [None] * buckets
        landed = []
        got_index = {}
        for t, s in enumerate(shifts):
            if answer_pick is None:
                message = jnp.concatenate(
                    [probe_bf, product[bucket_of[s]], index_rows[bucket_of[s]]], axis=0
                )
            else:
                message = jnp.concatenate([answers[t], product[bucket_of[s]]], axis=0)
            got = shifted_ring(message, "line", s)
            if answer_pick is None:
                fetched[bucket_of[-s]] = jnp.einsum(
                    "sk,kpr->spr",
                    far_pick[bucket_of[-s]],
                    got[:knots],
                    preferred_element_type=jnp.float32,
                ).astype(jnp.bfloat16)
                landed.append(got[knots : knots + slots])
                got_index[s] = got[knots + slots, 0, :slots].astype(jnp.float32)
            else:
                fetched[bucket_of[-s]] = got[:slots]
                landed.append(got[slots:])
        if answer_pick is None:
            answer_pick = jnp.concatenate(
                [(got_index[-s][:, None] == knot_vals[None, :]) for s in shifts], axis=0
            ).astype(jnp.bfloat16)
            land_place = jnp.concatenate(
                [(got_index[s][None, :] == knot_vals[:, None]) for s in shifts], axis=1
            ).astype(jnp.bfloat16)
        low = shifted_open(probe_bf[knots - 3 :], "seg", 1)
        high = shifted_open(probe_bf[:3], "seg", -1)
        stacked = jnp.concatenate(
            [low, probe_bf, high] + [fetched[b] for b in fetch_order], axis=0
        )
        summed = jnp.einsum(
            "kamb,mbr->kar", weight, stacked, preferred_element_type=jnp.float32
        )
        landed = jnp.concatenate(landed, axis=0)
        cross = jnp.einsum("ks,spr->kpr", land_place, landed, preferred_element_type=jnp.float32)
        residual = residual - (summed + cross)
        coeff_next = 1.0 / (2.0 * center / radius - coeff)
        direction = coeff_next * coeff * direction + 2.0 * coeff_next / radius * residual
        coeff = coeff_next
    return (solution + direction)[None]


def solution(mesh):
    return jax.shard_map(
        body,
        mesh=mesh,
        in_specs=(
            P("line", "seg", None, None),
            P("line", "seg", None, None, None),
            P("line", "seg", None, None, None),
            P("line", "seg", None),
            P("line", "seg", None, None, None, None),
        ),
        out_specs=P("line", "seg", None, None),
        check_vma=False,
    )
```

```python
import jax
import jax.numpy as jnp
from jax import lax
from jax.sharding import PartitionSpec as P

ITERS = 3


LO_BOUND = 1.5
HI_BOUND = 12.0


def shifted_open(value, axis, steps):
    count = lax.axis_size(axis)
    initial, last = (max(0, -steps), min(count, count - steps))
    return lax.ppermute(value, axis, [(source, source + steps) for source in range(initial, last)])


def shifted_ring(value, axis, steps):
    count = lax.axis_size(axis)
    return lax.ppermute(value, axis, [(i, (i + steps) % count) for i in range(count)])


def body(right_side, band_blocks, knot_pairs, pair_counts, cross_blocks):
    right_rows = right_side[0]
    blocks = band_blocks[0]
    my_pairs = knot_pairs[0, 0]
    used_count = pair_counts[0, 0]
    couplings = cross_blocks[0, 0]
    knots, params, probes = right_rows.shape
    buckets, slots = my_pairs.shape[0], my_pairs.shape[1]
    group_span = buckets // 2 + 1
    offsets = [
        b - (group_span - 1) if b < group_span - 1 else b - group_span + 2 for b in range(buckets)
    ]
    bucket_of = {o: b for b, o in enumerate(offsets)}
    shifts = [o for o in offsets if o > 0] + [o for o in offsets if o < 0]

    boundary_blocks = shifted_open(blocks[knots - 3 :], "seg", 1)
    lower_blocks = jnp.concatenate([boundary_blocks, blocks], axis=0)

    used = jnp.arange(slots, dtype=jnp.int32)[None, :] < used_count[:, None]
    own_knot = jnp.where(used, my_pairs[:, :, 0], -1)
    far_knot = jnp.where(used, my_pairs[:, :, 1], -1)
    knot_ids = jnp.arange(knots, dtype=jnp.int32)
    answer_knots = [None] * len(shifts)
    landing_knots = [None] * len(shifts)
    for t, s in enumerate(shifts):
        got = shifted_ring(far_knot[bucket_of[s]], "line", s)
        landing_knots[t] = got
        answer_knots[shifts.index(-s)] = got
    own_pick = (own_knot.reshape(-1)[:, None] == knot_ids[None, :]).astype(jnp.bfloat16)
    answer_pick = (jnp.concatenate(answer_knots)[:, None] == knot_ids[None, :]).astype(jnp.bfloat16)
    pick = jnp.concatenate([own_pick, answer_pick], axis=0)
    land_place = (jnp.concatenate(landing_knots)[None, :] == knot_ids[:, None]).astype(jnp.bfloat16)

    ext_knots = knots + 6
    band_col = jnp.arange(ext_knots, dtype=jnp.int32)[None, None, :, None]
    band_row = knot_ids[:, None, None, None]
    band_weight = jnp.zeros((knots, params, ext_knots, params), jnp.bfloat16)
    for step in range(4):
        band_weight = jnp.where(
            band_col == band_row + 3 + step, blocks[:, step][:, :, None, :], band_weight
        )
    for step in range(1, 4):
        flipped = jnp.swapaxes(lower_blocks[3 - step : 3 - step + knots, step], -1, -2)
        band_weight = jnp.where(band_col == band_row + 3 - step, flipped[:, :, None, :], band_weight)
    fetch_order = [bucket_of[-s] for s in shifts]
    fetch_knot = jnp.concatenate([own_knot[b] for b in fetch_order])
    fetch_blocks = jnp.concatenate([couplings[b] for b in fetch_order], axis=0)
    fetch_weight = jnp.where(
        fetch_knot[None, None, :, None] == knot_ids[:, None, None, None],
        jnp.swapaxes(fetch_blocks, 0, 1)[None],
        jnp.zeros((), jnp.bfloat16),
    )
    weight = jnp.concatenate([band_weight, fetch_weight], axis=2)

    center = (HI_BOUND + LO_BOUND) / 2.0
    radius = (HI_BOUND - LO_BOUND) / 2.0
    coeff = radius / center
    solution = jnp.zeros(right_rows.shape, jnp.float32)
    residual = right_rows
    direction = right_rows / center
    own_rows = buckets * slots
    for turn in range(ITERS):
        probe_bf = direction.astype(jnp.bfloat16)
        solution = solution + direction
        picked = jnp.einsum(
            "sk,kpr->spr", pick, probe_bf, preferred_element_type=jnp.float32
        ).astype(jnp.bfloat16)
        resident = picked[:own_rows].reshape(buckets, slots, params, probes)
        answers = picked[own_rows:].reshape(len(shifts), slots, params, probes)
        product = jnp.einsum(
            "bsqp,bsqr->bspr", couplings, resident, preferred_element_type=jnp.float32
        ).astype(jnp.bfloat16)
        fetched = [None] * buckets
        landed = []
        for t, s in enumerate(shifts):
            message = jnp.concatenate([answers[t], product[bucket_of[s]]], axis=0)
            got = shifted_ring(message, "line", s)
            fetched[bucket_of[-s]] = got[:slots]
            landed.append(got[slots:])
        low = shifted_open(probe_bf[knots - 3 :], "seg", 1)
        high = shifted_open(probe_bf[:3], "seg", -1)
        stacked = jnp.concatenate(
            [low, probe_bf, high] + [fetched[b] for b in fetch_order], axis=0
        )
        summed = jnp.einsum(
            "kamb,mbr->kar", weight, stacked, preferred_element_type=jnp.float32
        )
        landed = jnp.concatenate(landed, axis=0)
        cross = jnp.einsum("ks,spr->kpr", land_place, landed, preferred_element_type=jnp.float32)
        residual = residual - (summed + cross)
        coeff_next = 1.0 / (2.0 * center / radius - coeff)
        direction = coeff_next * coeff * direction + 2.0 * coeff_next / radius * residual
        coeff = coeff_next
    return (solution + direction)[None]


def solution(mesh):
    return jax.shard_map(
        body,
        mesh=mesh,
        in_specs=(
            P("line", "seg", None, None),
            P("line", "seg", None, None, None),
            P("line", "seg", None, None, None),
            P("line", "seg", None),
            P("line", "seg", None, None, None, None),
        ),
        out_specs=P("line", "seg", None, None),
        check_vma=False,
    )
```

```python
import jax
import jax.numpy as jnp
from jax import lax
from jax.sharding import PartitionSpec as P

ITERS = 3


LO_BOUND = 1.5
HI_BOUND = 12.0


def shifted_open(value, axis, steps):
    count = lax.axis_size(axis)
    initial, last = (max(0, -steps), min(count, count - steps))
    return lax.ppermute(value, axis, [(source, source + steps) for source in range(initial, last)])


def shifted_ring(value, axis, steps):
    count = lax.axis_size(axis)
    return lax.ppermute(value, axis, [(i, (i + steps) % count) for i in range(count)])


def body(right_side, band_blocks, knot_pairs, pair_counts, cross_blocks):
    right_rows = right_side[0]
    blocks = band_blocks[0]
    my_pairs = knot_pairs[0, 0]
    used_count = pair_counts[0, 0]
    couplings = cross_blocks[0, 0]
    knots, params, probes = right_rows.shape
    buckets, slots = my_pairs.shape[0], my_pairs.shape[1]
    group_span = buckets // 2 + 1
    offsets = [
        b - (group_span - 1) if b < group_span - 1 else b - group_span + 2 for b in range(buckets)
    ]
    bucket_of = {o: b for b, o in enumerate(offsets)}
    shifts = [o for o in offsets if o > 0] + [o for o in offsets if o < 0]

    center = (HI_BOUND + LO_BOUND) / 2.0
    first_direction = right_rows / center
    first_probe = first_direction.astype(jnp.bfloat16)
    tail_blocks = blocks[knots - 3 :]
    tail_probe = first_probe[knots - 3 :]
    sent_down = shifted_open(
        jnp.concatenate([tail_blocks.reshape(-1), tail_probe.reshape(-1)]), "seg", 1
    )
    boundary_blocks = sent_down[: tail_blocks.size].reshape(tail_blocks.shape)
    first_low = sent_down[tail_blocks.size :].reshape(tail_probe.shape)
    lower_blocks = jnp.concatenate([boundary_blocks, blocks], axis=0)

    used = jnp.arange(slots, dtype=jnp.int32)[None, :] < used_count[:, None]
    own_knot = jnp.where(used, my_pairs[:, :, 0], -1)
    far_knot = jnp.where(used, my_pairs[:, :, 1], -1)
    knot_ids = jnp.arange(knots, dtype=jnp.int32)
    own_pick = (own_knot.reshape(-1)[:, None] == knot_ids[None, :]).astype(jnp.bfloat16)
    own_place = (own_knot.reshape(-1)[None, :] == knot_ids[:, None]).astype(jnp.float32)
    far_pick = (far_knot[:, :, None] == knot_ids[None, None, :]).astype(jnp.bfloat16)
    index_rows = jnp.zeros((buckets, 1, params, probes), jnp.bfloat16)
    index_rows = index_rows.at[:, 0, 0, :slots].set(far_knot.astype(jnp.bfloat16))
    knot_vals = knot_ids.astype(jnp.float32)
    ext_knots = knots + 6
    ext_ids = jnp.arange(ext_knots, dtype=jnp.int32)
    band_weight = None
    for step in range(4):
        place = (ext_ids[None, :] == knot_ids[:, None] + 3 + step).astype(jnp.float32)
        term = jnp.einsum("km,kab->kamb", place, blocks[:, step].astype(jnp.float32))
        band_weight = term if band_weight is None else band_weight + term
    for step in range(1, 4):
        place = (ext_ids[None, :] == knot_ids[:, None] + 3 - step).astype(jnp.float32)
        band_weight = band_weight + jnp.einsum(
            "km,kba->kamb", place, lower_blocks[3 - step : 3 - step + knots, step].astype(jnp.float32)
        )
    fetch_order = [bucket_of[-s] for s in shifts]
    fetch_place = jnp.concatenate(
        [own_place.reshape(knots, buckets, slots)[:, b] for b in fetch_order], axis=1
    )
    fetch_blocks = jnp.concatenate([couplings[b] for b in fetch_order], axis=0).astype(jnp.float32)
    fetch_weight = jnp.einsum("kf,fab->kafb", fetch_place, fetch_blocks)
    weight = jnp.concatenate([band_weight, fetch_weight], axis=2).astype(jnp.bfloat16)
    answer_pick = None
    land_place = None

    center = (HI_BOUND + LO_BOUND) / 2.0
    radius = (HI_BOUND - LO_BOUND) / 2.0
    coeff = radius / center
    solution = jnp.zeros(right_rows.shape, jnp.float32)
    residual = right_rows
    direction = first_direction
    own_rows = buckets * slots
    for turn in range(ITERS):
        probe_bf = first_probe if turn == 0 else direction.astype(jnp.bfloat16)
        solution = solution + direction
        if answer_pick is None:
            picked = jnp.einsum(
                "sk,kpr->spr", own_pick, probe_bf, preferred_element_type=jnp.float32
            ).astype(jnp.bfloat16)
            resident = picked.reshape(buckets, slots, params, probes)
        else:
            picked = jnp.einsum(
                "sk,kpr->spr",
                jnp.concatenate([own_pick, answer_pick], axis=0),
                probe_bf,
                preferred_element_type=jnp.float32,
            ).astype(jnp.bfloat16)
            resident = picked[:own_rows].reshape(buckets, slots, params, probes)
            answers = picked[own_rows:].reshape(len(shifts), slots, params, probes)
        product = jnp.einsum(
            "bsqp,bsqr->bspr", couplings, resident, preferred_element_type=jnp.float32
        ).astype(jnp.bfloat16)
        fetched = [None] * buckets
        landed = []
        got_index = {}
        for t, s in enumerate(shifts):
            if answer_pick is None:
                message = jnp.concatenate(
                    [probe_bf, product[bucket_of[s]], index_rows[bucket_of[s]]], axis=0
                )
            else:
                message = jnp.concatenate([answers[t], product[bucket_of[s]]], axis=0)
            got = shifted_ring(message, "line", s)
            if answer_pick is None:
                fetched[bucket_of[-s]] = jnp.einsum(
                    "sk,kpr->spr",
                    far_pick[bucket_of[-s]],
                    got[:knots],
                    preferred_element_type=jnp.float32,
                ).astype(jnp.bfloat16)
                landed.append(got[knots : knots + slots])
                got_index[s] = got[knots + slots, 0, :slots].astype(jnp.float32)
            else:
                fetched[bucket_of[-s]] = got[:slots]
                landed.append(got[slots:])
        if answer_pick is None:
            answer_pick = jnp.concatenate(
                [(got_index[-s][:, None] == knot_vals[None, :]) for s in shifts], axis=0
            ).astype(jnp.bfloat16)
            land_place = jnp.concatenate(
                [(got_index[s][None, :] == knot_vals[:, None]) for s in shifts], axis=1
            ).astype(jnp.bfloat16)
        low = first_low if turn == 0 else shifted_open(probe_bf[knots - 3 :], "seg", 1)
        high = shifted_open(probe_bf[:3], "seg", -1)
        stacked = jnp.concatenate(
            [low, probe_bf, high] + [fetched[b] for b in fetch_order], axis=0
        )
        summed = jnp.einsum(
            "kamb,mbr->kar", weight, stacked, preferred_element_type=jnp.float32
        )
        landed = jnp.concatenate(landed, axis=0)
        cross = jnp.einsum("ks,spr->kpr", land_place, landed, preferred_element_type=jnp.float32)
        residual = residual - (summed + cross)
        coeff_next = 1.0 / (2.0 * center / radius - coeff)
        direction = coeff_next * coeff * direction + 2.0 * coeff_next / radius * residual
        coeff = coeff_next
    return (solution + direction)[None]


def solution(mesh):
    return jax.shard_map(
        body,
        mesh=mesh,
        in_specs=(
            P("line", "seg", None, None),
            P("line", "seg", None, None, None),
            P("line", "seg", None, None, None),
            P("line", "seg", None),
            P("line", "seg", None, None, None, None),
        ),
        out_specs=P("line", "seg", None, None),
        check_vma=False,
    )
```

```python
import jax
import jax.numpy as jnp
from jax import lax
from jax.sharding import PartitionSpec as P
from jax.experimental import pallas as pl
from jax.experimental.pallas import tpu as pltpu

ITERS = 3


LO_BOUND = 1.5
HI_BOUND = 12.0


def shifted_open(value, axis, steps):
    count = lax.axis_size(axis)
    initial, last = (max(0, -steps), min(count, count - steps))
    return lax.ppermute(value, axis, [(source, source + steps) for source in range(initial, last)])


def shifted_ring(value, axis, steps):
    count = lax.axis_size(axis)
    return lax.ppermute(value, axis, [(i, (i + steps) % count) for i in range(count)])


def unpack_first(pick_ref, low_ref, probe_ref, high_ref, *refs):
    messages = refs[:-3]
    stacked_ref, landed_ref, index_ref = refs[-3:]
    edge = low_ref.shape[0]
    knots = probe_ref.shape[0]
    slots = pick_ref.shape[1]
    stacked_ref[:edge] = low_ref[...]
    stacked_ref[edge : edge + knots] = probe_ref[...]
    stacked_ref[edge + knots : 2 * edge + knots] = high_ref[...]
    base = 2 * edge + knots
    for t, message in enumerate(messages):
        for slot in range(slots):
            knot = pick_ref[t, slot]
            row = message[jnp.minimum(jnp.maximum(knot, 0), knots - 1)]
            stacked_ref[base + t * slots + slot] = jnp.where(knot >= 0, row, jnp.zeros_like(row))
            landed_ref[t * slots + slot] = message[knots + slot]
        index_ref[t] = message[knots + slots, 0, :]


def unpack_call(pick, low, probe, high, messages):
    knots, params, probes = probe.shape
    slots = pick.shape[1]
    count = len(messages)
    vmem = pl.BlockSpec(memory_space=pltpu.VMEM)
    return pl.pallas_call(
        unpack_first,
        out_shape=(
            jax.ShapeDtypeStruct((knots + 2 * low.shape[0] + count * slots, params, probes), probe.dtype),
            jax.ShapeDtypeStruct((count * slots, params, probes), probe.dtype),
            jax.ShapeDtypeStruct((count, probes), probe.dtype),
        ),
        in_specs=[pl.BlockSpec(memory_space=pltpu.SMEM)] + [vmem] * (3 + count),
        out_specs=(vmem, vmem, vmem),
    )(pick, low, probe, high, *messages)


def body(right_side, band_blocks, knot_pairs, pair_counts, cross_blocks):
    right_rows = right_side[0]
    blocks = band_blocks[0]
    my_pairs = knot_pairs[0, 0]
    used_count = pair_counts[0, 0]
    couplings = cross_blocks[0, 0]
    knots, params, probes = right_rows.shape
    buckets, slots = my_pairs.shape[0], my_pairs.shape[1]
    group_span = buckets // 2 + 1
    offsets = [
        b - (group_span - 1) if b < group_span - 1 else b - group_span + 2 for b in range(buckets)
    ]
    bucket_of = {o: b for b, o in enumerate(offsets)}
    shifts = [o for o in offsets if o > 0] + [o for o in offsets if o < 0]

    boundary_blocks = shifted_open(blocks[knots - 3 :], "seg", 1)
    lower_blocks = jnp.concatenate([boundary_blocks, blocks], axis=0)

    used = jnp.arange(slots, dtype=jnp.int32)[None, :] < used_count[:, None]
    own_knot = jnp.where(used, my_pairs[:, :, 0], -1)
    far_knot = jnp.where(used, my_pairs[:, :, 1], -1)
    knot_ids = jnp.arange(knots, dtype=jnp.int32)
    own_pick = (own_knot.reshape(-1)[:, None] == knot_ids[None, :]).astype(jnp.bfloat16)
    own_place = (own_knot.reshape(-1)[None, :] == knot_ids[:, None]).astype(jnp.float32)
    far_pick = (far_knot[:, :, None] == knot_ids[None, None, :]).astype(jnp.bfloat16)
    index_rows = jnp.zeros((buckets, 1, params, probes), jnp.bfloat16)
    index_rows = index_rows.at[:, 0, 0, :slots].set(far_knot.astype(jnp.bfloat16))
    knot_vals = knot_ids.astype(jnp.float32)
    ext_knots = knots + 6
    ext_ids = jnp.arange(ext_knots, dtype=jnp.int32)
    band_weight = None
    for step in range(4):
        place = (ext_ids[None, :] == knot_ids[:, None] + 3 + step).astype(jnp.float32)
        term = jnp.einsum("km,kab->kamb", place, blocks[:, step].astype(jnp.float32))
        band_weight = term if band_weight is None else band_weight + term
    for step in range(1, 4):
        place = (ext_ids[None, :] == knot_ids[:, None] + 3 - step).astype(jnp.float32)
        band_weight = band_weight + jnp.einsum(
            "km,kba->kamb", place, lower_blocks[3 - step : 3 - step + knots, step].astype(jnp.float32)
        )
    fetch_order = [bucket_of[-s] for s in shifts]
    fetch_place = jnp.concatenate(
        [own_place.reshape(knots, buckets, slots)[:, b] for b in fetch_order], axis=1
    )
    fetch_blocks = jnp.concatenate([couplings[b] for b in fetch_order], axis=0).astype(jnp.float32)
    fetch_weight = jnp.einsum("kf,fab->kafb", fetch_place, fetch_blocks)
    weight = jnp.concatenate([band_weight, fetch_weight], axis=2).astype(jnp.bfloat16)
    first_pick = jnp.stack([far_knot[bucket_of[-s]] for s in shifts])
    answer_pick = None
    land_place = None

    center = (HI_BOUND + LO_BOUND) / 2.0
    radius = (HI_BOUND - LO_BOUND) / 2.0
    coeff = radius / center
    solution = jnp.zeros(right_rows.shape, jnp.float32)
    residual = right_rows
    direction = right_rows / center
    own_rows = buckets * slots
    for turn in range(ITERS):
        probe_bf = direction.astype(jnp.bfloat16)
        solution = solution + direction
        if answer_pick is None:
            picked = jnp.einsum(
                "sk,kpr->spr", own_pick, probe_bf, preferred_element_type=jnp.float32
            ).astype(jnp.bfloat16)
            resident = picked.reshape(buckets, slots, params, probes)
        else:
            picked = jnp.einsum(
                "sk,kpr->spr",
                jnp.concatenate([own_pick, answer_pick], axis=0),
                probe_bf,
                preferred_element_type=jnp.float32,
            ).astype(jnp.bfloat16)
            resident = picked[:own_rows].reshape(buckets, slots, params, probes)
            answers = picked[own_rows:].reshape(len(shifts), slots, params, probes)
        product = jnp.einsum(
            "bsqp,bsqr->bspr", couplings, resident, preferred_element_type=jnp.float32
        ).astype(jnp.bfloat16)
        fetched = [None] * buckets
        landed = []
        received = []
        for t, s in enumerate(shifts):
            if answer_pick is None:
                message = jnp.concatenate(
                    [probe_bf, product[bucket_of[s]], index_rows[bucket_of[s]]], axis=0
                )
            else:
                message = jnp.concatenate([answers[t], product[bucket_of[s]]], axis=0)
            got = shifted_ring(message, "line", s)
            received.append(got)
            fetched[bucket_of[-s]] = got[:slots]
            landed.append(got[slots:])
        low = shifted_open(probe_bf[knots - 3 :], "seg", 1)
        high = shifted_open(probe_bf[:3], "seg", -1)
        if answer_pick is None:
            stacked, landed, heard = unpack_call(first_pick, low, probe_bf, high, received)
            heard = heard[:, :slots].astype(jnp.float32)
            answer_pick = jnp.concatenate(
                [(heard[shifts.index(-s)][:, None] == knot_vals[None, :]) for s in shifts], axis=0
            ).astype(jnp.bfloat16)
            land_place = (heard.reshape(-1)[None, :] == knot_vals[:, None]).astype(jnp.bfloat16)
        else:
            stacked = jnp.concatenate(
                [low, probe_bf, high] + [fetched[b] for b in fetch_order], axis=0
            )
            landed = jnp.concatenate(landed, axis=0)
        summed = jnp.einsum(
            "kamb,mbr->kar", weight, stacked, preferred_element_type=jnp.float32
        )
        cross = jnp.einsum("ks,spr->kpr", land_place, landed, preferred_element_type=jnp.float32)
        residual = residual - (summed + cross)
        coeff_next = 1.0 / (2.0 * center / radius - coeff)
        direction = coeff_next * coeff * direction + 2.0 * coeff_next / radius * residual
        coeff = coeff_next
    return (solution + direction)[None]


def solution(mesh):
    return jax.shard_map(
        body,
        mesh=mesh,
        in_specs=(
            P("line", "seg", None, None),
            P("line", "seg", None, None, None),
            P("line", "seg", None, None, None),
            P("line", "seg", None),
            P("line", "seg", None, None, None, None),
        ),
        out_specs=P("line", "seg", None, None),
        check_vma=False,
    )
```

```python
import jax
import jax.numpy as jnp
from jax import lax
from jax.sharding import PartitionSpec as P
from jax.experimental import pallas as pl
from jax.experimental.pallas import tpu as pltpu

ITERS = 3


LO_BOUND = 1.5
HI_BOUND = 12.0


def shifted_open(value, axis, steps):
    count = lax.axis_size(axis)
    initial, last = (max(0, -steps), min(count, count - steps))
    return lax.ppermute(value, axis, [(source, source + steps) for source in range(initial, last)])


def shifted_ring(value, axis, steps):
    count = lax.axis_size(axis)
    return lax.ppermute(value, axis, [(i, (i + steps) % count) for i in range(count)])


def unpack_first(pick_ref, low_ref, probe_ref, high_ref, *refs):
    messages = refs[:-3]
    stacked_ref, landed_ref, index_ref = refs[-3:]
    edge = low_ref.shape[0]
    knots = probe_ref.shape[0]
    slots = pick_ref.shape[1]
    stacked_ref[:edge] = low_ref[...]
    stacked_ref[edge : edge + knots] = probe_ref[...]
    stacked_ref[edge + knots : 2 * edge + knots] = high_ref[...]
    base = 2 * edge + knots
    for t, message in enumerate(messages):
        for slot in range(slots):
            knot = pick_ref[t, slot]
            row = message[jnp.minimum(jnp.maximum(knot, 0), knots - 1)]
            stacked_ref[base + t * slots + slot] = jnp.where(knot >= 0, row, jnp.zeros_like(row))
            landed_ref[t * slots + slot] = message[knots + slot]
        index_ref[t] = message[knots + slots, 0, :]


def unpack_call(pick, low, probe, high, messages):
    knots, params, probes = probe.shape
    slots = pick.shape[1]
    count = len(messages)
    vmem = pl.BlockSpec(memory_space=pltpu.VMEM)
    return pl.pallas_call(
        unpack_first,
        out_shape=(
            jax.ShapeDtypeStruct((knots + 2 * low.shape[0] + count * slots, params, probes), probe.dtype),
            jax.ShapeDtypeStruct((count * slots, params, probes), probe.dtype),
            jax.ShapeDtypeStruct((count, probes), probe.dtype),
        ),
        in_specs=[pl.BlockSpec(memory_space=pltpu.SMEM)] + [vmem] * (3 + count),
        out_specs=(vmem, vmem, vmem),
    )(pick, low, probe, high, *messages)


def body(right_side, band_blocks, knot_pairs, pair_counts, cross_blocks):
    right_rows = right_side[0]
    blocks = band_blocks[0]
    my_pairs = knot_pairs[0, 0]
    used_count = pair_counts[0, 0]
    couplings = cross_blocks[0, 0]
    knots, params, probes = right_rows.shape
    buckets, slots = my_pairs.shape[0], my_pairs.shape[1]
    group_span = buckets // 2 + 1
    offsets = [
        b - (group_span - 1) if b < group_span - 1 else b - group_span + 2 for b in range(buckets)
    ]
    bucket_of = {o: b for b, o in enumerate(offsets)}
    shifts = [o for o in offsets if o < 0][::-1] + [o for o in offsets if o > 0]

    boundary_blocks = shifted_open(blocks[knots - 3 :], "seg", 1)
    lower_blocks = jnp.concatenate([boundary_blocks, blocks], axis=0)

    used = jnp.arange(slots, dtype=jnp.int32)[None, :] < used_count[:, None]
    own_knot = jnp.where(used, my_pairs[:, :, 0], -1)
    far_knot = jnp.where(used, my_pairs[:, :, 1], -1)
    knot_ids = jnp.arange(knots, dtype=jnp.int32)
    own_pick = (own_knot.reshape(-1)[:, None] == knot_ids[None, :]).astype(jnp.bfloat16)
    own_place = (own_knot.reshape(-1)[None, :] == knot_ids[:, None]).astype(jnp.float32)
    far_pick = (far_knot[:, :, None] == knot_ids[None, None, :]).astype(jnp.bfloat16)
    index_rows = jnp.zeros((buckets, 1, params, probes), jnp.bfloat16)
    index_rows = index_rows.at[:, 0, 0, :slots].set(far_knot.astype(jnp.bfloat16))
    knot_vals = knot_ids.astype(jnp.float32)
    ext_knots = knots + 6
    ext_ids = jnp.arange(ext_knots, dtype=jnp.int32)
    band_weight = None
    for step in range(4):
        place = (ext_ids[None, :] == knot_ids[:, None] + 3 + step).astype(jnp.float32)
        term = jnp.einsum("km,kab->kamb", place, blocks[:, step].astype(jnp.float32))
        band_weight = term if band_weight is None else band_weight + term
    for step in range(1, 4):
        place = (ext_ids[None, :] == knot_ids[:, None] + 3 - step).astype(jnp.float32)
        flipped = jnp.swapaxes(lower_blocks[3 - step : 3 - step + knots, step], -1, -2)
        band_weight = band_weight + jnp.einsum("km,kab->kamb", place, flipped.astype(jnp.float32))
    fetch_order = [bucket_of[-s] for s in shifts]
    fetch_place = jnp.concatenate(
        [own_place.reshape(knots, buckets, slots)[:, b] for b in fetch_order], axis=1
    )
    fetch_blocks = jnp.concatenate([couplings[b] for b in fetch_order], axis=0).astype(jnp.float32)
    fetch_weight = jnp.einsum("kf,fab->kafb", fetch_place, fetch_blocks)
    weight = jnp.concatenate([band_weight, fetch_weight], axis=2).astype(jnp.bfloat16)
    first_pick = jnp.stack([far_knot[bucket_of[-s]] for s in shifts])
    answer_pick = None
    land_place = None

    center = (HI_BOUND + LO_BOUND) / 2.0
    radius = (HI_BOUND - LO_BOUND) / 2.0
    coeff = radius / center
    solution = jnp.zeros(right_rows.shape, jnp.float32)
    residual = right_rows
    direction = right_rows / center
    own_rows = buckets * slots
    for turn in range(ITERS):
        probe_bf = direction.astype(jnp.bfloat16)
        solution = solution + direction
        if answer_pick is None:
            picked = jnp.einsum(
                "sk,kpr->spr", own_pick, probe_bf, preferred_element_type=jnp.float32
            ).astype(jnp.bfloat16)
            resident = picked.reshape(buckets, slots, params, probes)
        else:
            picked = jnp.einsum(
                "sk,kpr->spr",
                jnp.concatenate([own_pick, answer_pick], axis=0),
                probe_bf,
                preferred_element_type=jnp.float32,
            ).astype(jnp.bfloat16)
            resident = picked[:own_rows].reshape(buckets, slots, params, probes)
            answers = picked[own_rows:].reshape(len(shifts), slots, params, probes)
        product = jnp.einsum(
            "bsqp,bsqr->bspr", couplings, resident, preferred_element_type=jnp.float32
        ).astype(jnp.bfloat16)
        fetched = [None] * buckets
        landed = []
        received = []
        for t, s in enumerate(shifts):
            if answer_pick is None:
                message = jnp.concatenate(
                    [probe_bf, product[bucket_of[s]], index_rows[bucket_of[s]]], axis=0
                )
            else:
                message = jnp.concatenate([answers[t], product[bucket_of[s]]], axis=0)
            got = shifted_ring(message, "line", s)
            received.append(got)
            fetched[bucket_of[-s]] = got[:slots]
            landed.append(got[slots:])
        low = shifted_open(probe_bf[knots - 3 :], "seg", 1)
        high = shifted_open(probe_bf[:3], "seg", -1)
        if answer_pick is None:
            stacked, landed, heard = unpack_call(first_pick, low, probe_bf, high, received)
            heard = heard[:, :slots].astype(jnp.float32)
            answer_pick = jnp.concatenate(
                [(heard[shifts.index(-s)][:, None] == knot_vals[None, :]) for s in shifts], axis=0
            ).astype(jnp.bfloat16)
            land_place = (heard.reshape(-1)[None, :] == knot_vals[:, None]).astype(jnp.bfloat16)
        else:
            stacked = jnp.concatenate(
                [low, probe_bf, high] + [fetched[b] for b in fetch_order], axis=0
            )
            landed = jnp.concatenate(landed, axis=0)
        summed = jnp.einsum(
            "kamb,mbr->kar", weight, stacked, preferred_element_type=jnp.float32
        )
        cross = jnp.einsum("ks,spr->kpr", land_place, landed, preferred_element_type=jnp.float32)
        residual = residual - (summed + cross)
        coeff_next = 1.0 / (2.0 * center / radius - coeff)
        direction = coeff_next * coeff * direction + 2.0 * coeff_next / radius * residual
        coeff = coeff_next
    return (solution + direction)[None]


def solution(mesh):
    return jax.shard_map(
        body,
        mesh=mesh,
        in_specs=(
            P("line", "seg", None, None),
            P("line", "seg", None, None, None),
            P("line", "seg", None, None, None),
            P("line", "seg", None),
            P("line", "seg", None, None, None, None),
        ),
        out_specs=P("line", "seg", None, None),
        check_vma=False,
    )
```

```python
import jax
import jax.numpy as jnp
from jax import lax
from jax.sharding import PartitionSpec as P
from jax.experimental import pallas as pl
from jax.experimental.pallas import tpu as pltpu

ITERS = 3


LO_BOUND = 1.5
HI_BOUND = 12.0


def shifted_open(value, axis, steps):
    count = lax.axis_size(axis)
    initial, last = (max(0, -steps), min(count, count - steps))
    return lax.ppermute(value, axis, [(source, source + steps) for source in range(initial, last)])


def shifted_ring(value, axis, steps):
    count = lax.axis_size(axis)
    return lax.ppermute(value, axis, [(i, (i + steps) % count) for i in range(count)])


def unpack_first(pick_ref, low_ref, probe_ref, high_ref, *refs):
    messages = refs[:-3]
    stacked_ref, landed_ref, index_ref = refs[-3:]
    edge = low_ref.shape[0]
    knots = probe_ref.shape[0]
    slots = pick_ref.shape[1]
    stacked_ref[:edge] = low_ref[...]
    stacked_ref[edge : edge + knots] = probe_ref[...]
    stacked_ref[edge + knots : 2 * edge + knots] = high_ref[...]
    base = 2 * edge + knots
    for t, message in enumerate(messages):
        for slot in range(slots):
            knot = pick_ref[t, slot]
            row = message[jnp.minimum(jnp.maximum(knot, 0), knots - 1)]
            stacked_ref[base + t * slots + slot] = jnp.where(knot >= 0, row, jnp.zeros_like(row))
            landed_ref[t * slots + slot] = message[knots + slot]
        index_ref[t] = message[knots + slots, 0, :]


def unpack_call(pick, low, probe, high, messages):
    knots, params, probes = probe.shape
    slots = pick.shape[1]
    count = len(messages)
    vmem = pl.BlockSpec(memory_space=pltpu.VMEM)
    return pl.pallas_call(
        unpack_first,
        out_shape=(
            jax.ShapeDtypeStruct((knots + 2 * low.shape[0] + count * slots, params, probes), probe.dtype),
            jax.ShapeDtypeStruct((count * slots, params, probes), probe.dtype),
            jax.ShapeDtypeStruct((count, probes), probe.dtype),
        ),
        in_specs=[pl.BlockSpec(memory_space=pltpu.SMEM)] + [vmem] * (3 + count),
        out_specs=(vmem, vmem, vmem),
    )(pick, low, probe, high, *messages)


def body(right_side, band_blocks, knot_pairs, pair_counts, cross_blocks):
    right_rows = right_side[0]
    blocks = band_blocks[0]
    my_pairs = knot_pairs[0, 0]
    used_count = pair_counts[0, 0]
    couplings = cross_blocks[0, 0]
    knots, params, probes = right_rows.shape
    buckets, slots = my_pairs.shape[0], my_pairs.shape[1]
    group_span = buckets // 2 + 1
    offsets = [
        b - (group_span - 1) if b < group_span - 1 else b - group_span + 2 for b in range(buckets)
    ]
    bucket_of = {o: b for b, o in enumerate(offsets)}
    shifts = [o for o in offsets if o > 0] + [o for o in offsets if o < 0]

    boundary_blocks = shifted_open(blocks[knots - 3 :], "seg", 1)
    lower_blocks = jnp.concatenate([boundary_blocks, blocks], axis=0)

    used = jnp.arange(slots, dtype=jnp.int32)[None, :] < used_count[:, None]
    own_knot = jnp.where(used, my_pairs[:, :, 0], -1)
    far_knot = jnp.where(used, my_pairs[:, :, 1], -1)
    knot_ids = jnp.arange(knots, dtype=jnp.int32)
    own_pick = (own_knot.reshape(-1)[:, None] == knot_ids[None, :]).astype(jnp.bfloat16)
    own_place = (own_knot.reshape(-1)[None, :] == knot_ids[:, None]).astype(jnp.float32)
    far_pick = (far_knot[:, :, None] == knot_ids[None, None, :]).astype(jnp.bfloat16)
    index_rows = jnp.zeros((buckets, 1, params, probes), jnp.bfloat16)
    index_rows = index_rows.at[:, 0, 0, :slots].set(far_knot.astype(jnp.bfloat16))
    knot_vals = knot_ids.astype(jnp.float32)
    ext_knots = knots + 6
    ext_ids = jnp.arange(ext_knots, dtype=jnp.int32)
    band_weight = None
    for step in range(4):
        place = (ext_ids[None, :] == knot_ids[:, None] + 3 + step).astype(jnp.bfloat16)
        term = jnp.einsum("km,kab->kamb", place, blocks[:, step], preferred_element_type=jnp.bfloat16)
        band_weight = term if band_weight is None else band_weight + term
    for step in range(1, 4):
        place = (ext_ids[None, :] == knot_ids[:, None] + 3 - step).astype(jnp.bfloat16)
        band_weight = band_weight + jnp.einsum(
            "km,kba->kamb",
            place,
            lower_blocks[3 - step : 3 - step + knots, step],
            preferred_element_type=jnp.bfloat16,
        )
    fetch_order = [bucket_of[-s] for s in shifts]
    fetch_place = jnp.concatenate(
        [own_place.reshape(knots, buckets, slots)[:, b] for b in fetch_order], axis=1
    )
    fetch_blocks = jnp.concatenate([couplings[b] for b in fetch_order], axis=0)
    fetch_weight = jnp.einsum(
        "kf,fab->kafb", fetch_place.astype(jnp.bfloat16), fetch_blocks, preferred_element_type=jnp.bfloat16
    )
    weight = jnp.concatenate([band_weight, fetch_weight], axis=2)
    first_pick = jnp.stack([far_knot[bucket_of[-s]] for s in shifts])
    answer_pick = None
    land_place = None

    center = (HI_BOUND + LO_BOUND) / 2.0
    radius = (HI_BOUND - LO_BOUND) / 2.0
    coeff = radius / center
    solution = jnp.zeros(right_rows.shape, jnp.float32)
    residual = right_rows
    direction = right_rows / center
    own_rows = buckets * slots
    for turn in range(ITERS):
        probe_bf = direction.astype(jnp.bfloat16)
        solution = solution + direction
        if answer_pick is None:
            picked = jnp.einsum(
                "sk,kpr->spr", own_pick, probe_bf, preferred_element_type=jnp.float32
            ).astype(jnp.bfloat16)
            resident = picked.reshape(buckets, slots, params, probes)
        else:
            picked = jnp.einsum(
                "sk,kpr->spr",
                jnp.concatenate([own_pick, answer_pick], axis=0),
                probe_bf,
                preferred_element_type=jnp.float32,
            ).astype(jnp.bfloat16)
            resident = picked[:own_rows].reshape(buckets, slots, params, probes)
            answers = picked[own_rows:].reshape(len(shifts), slots, params, probes)
        product = jnp.einsum(
            "bsqp,bsqr->bspr", couplings, resident, preferred_element_type=jnp.float32
        ).astype(jnp.bfloat16)
        fetched = [None] * buckets
        landed = []
        received = []
        for t, s in enumerate(shifts):
            if answer_pick is None:
                message = jnp.concatenate(
                    [probe_bf, product[bucket_of[s]], index_rows[bucket_of[s]]], axis=0
                )
            else:
                message = jnp.concatenate([answers[t], product[bucket_of[s]]], axis=0)
            got = shifted_ring(message, "line", s)
            received.append(got)
            fetched[bucket_of[-s]] = got[:slots]
            landed.append(got[slots:])
        low = shifted_open(probe_bf[knots - 3 :], "seg", 1)
        high = shifted_open(probe_bf[:3], "seg", -1)
        if answer_pick is None:
            stacked, landed, heard = unpack_call(first_pick, low, probe_bf, high, received)
            heard = heard[:, :slots].astype(jnp.float32)
            answer_pick = jnp.concatenate(
                [(heard[shifts.index(-s)][:, None] == knot_vals[None, :]) for s in shifts], axis=0
            ).astype(jnp.bfloat16)
            land_place = (heard.reshape(-1)[None, :] == knot_vals[:, None]).astype(jnp.bfloat16)
        else:
            stacked = jnp.concatenate(
                [low, probe_bf, high] + [fetched[b] for b in fetch_order], axis=0
            )
            landed = jnp.concatenate(landed, axis=0)
        summed = jnp.einsum(
            "kamb,mbr->kar", weight, stacked, preferred_element_type=jnp.float32
        )
        cross = jnp.einsum("ks,spr->kpr", land_place, landed, preferred_element_type=jnp.float32)
        residual = residual - (summed + cross)
        coeff_next = 1.0 / (2.0 * center / radius - coeff)
        direction = coeff_next * coeff * direction + 2.0 * coeff_next / radius * residual
        coeff = coeff_next
    return (solution + direction)[None]


def solution(mesh):
    return jax.shard_map(
        body,
        mesh=mesh,
        in_specs=(
            P("line", "seg", None, None),
            P("line", "seg", None, None, None),
            P("line", "seg", None, None, None),
            P("line", "seg", None),
            P("line", "seg", None, None, None, None),
        ),
        out_specs=P("line", "seg", None, None),
        check_vma=False,
    )
```

```python
import jax
import jax.numpy as jnp
from jax import lax
from jax.sharding import PartitionSpec as P
from jax.experimental import pallas as pl
from jax.experimental.pallas import tpu as pltpu

ITERS = 3


LO_BOUND = 1.5
HI_BOUND = 12.0


def shifted_open(value, axis, steps):
    count = lax.axis_size(axis)
    initial, last = (max(0, -steps), min(count, count - steps))
    return lax.ppermute(value, axis, [(source, source + steps) for source in range(initial, last)])


def shifted_ring(value, axis, steps):
    count = lax.axis_size(axis)
    return lax.ppermute(value, axis, [(i, (i + steps) % count) for i in range(count)])


def unpack_first(pick_ref, *refs):
    messages = refs[:-3]
    fetched_ref, landed_ref, index_ref = refs[-3:]
    slots = pick_ref.shape[1]
    knots = messages[0].shape[0] - slots - 1
    for t, message in enumerate(messages):
        for slot in range(slots):
            knot = pick_ref[t, slot]
            row = message[jnp.minimum(jnp.maximum(knot, 0), knots - 1)]
            fetched_ref[t * slots + slot] = jnp.where(knot >= 0, row, jnp.zeros_like(row))
            landed_ref[t * slots + slot] = message[knots + slot]
        index_ref[t] = message[knots + slots, 0, :]


def unpack_call(pick, messages):
    rows, params, probes = messages[0].shape
    slots = pick.shape[1]
    count = len(messages)
    vmem = pl.BlockSpec(memory_space=pltpu.VMEM)
    return pl.pallas_call(
        unpack_first,
        out_shape=(
            jax.ShapeDtypeStruct((count * slots, params, probes), messages[0].dtype),
            jax.ShapeDtypeStruct((count * slots, params, probes), messages[0].dtype),
            jax.ShapeDtypeStruct((count, probes), messages[0].dtype),
        ),
        in_specs=[pl.BlockSpec(memory_space=pltpu.SMEM)] + [vmem] * count,
        out_specs=(vmem, vmem, vmem),
    )(pick, *messages)


def body(right_side, band_blocks, knot_pairs, pair_counts, cross_blocks):
    right_rows = right_side[0]
    blocks = band_blocks[0]
    my_pairs = knot_pairs[0, 0]
    used_count = pair_counts[0, 0]
    couplings = cross_blocks[0, 0]
    knots, params, probes = right_rows.shape
    buckets, slots = my_pairs.shape[0], my_pairs.shape[1]
    group_span = buckets // 2 + 1
    offsets = [
        b - (group_span - 1) if b < group_span - 1 else b - group_span + 2 for b in range(buckets)
    ]
    bucket_of = {o: b for b, o in enumerate(offsets)}
    shifts = [o for o in offsets if o > 0] + [o for o in offsets if o < 0]

    boundary_blocks = shifted_open(blocks[knots - 3 :], "seg", 1)
    lower_blocks = jnp.concatenate([boundary_blocks, blocks], axis=0)

    used = jnp.arange(slots, dtype=jnp.int32)[None, :] < used_count[:, None]
    own_knot = jnp.where(used, my_pairs[:, :, 0], -1)
    far_knot = jnp.where(used, my_pairs[:, :, 1], -1)
    knot_ids = jnp.arange(knots, dtype=jnp.int32)
    own_pick = (own_knot.reshape(-1)[:, None] == knot_ids[None, :]).astype(jnp.bfloat16)
    own_place = (own_knot.reshape(-1)[None, :] == knot_ids[:, None]).astype(jnp.float32)
    far_pick = (far_knot[:, :, None] == knot_ids[None, None, :]).astype(jnp.bfloat16)
    index_rows = jnp.zeros((buckets, 1, params, probes), jnp.bfloat16)
    index_rows = index_rows.at[:, 0, 0, :slots].set(far_knot.astype(jnp.bfloat16))
    knot_vals = knot_ids.astype(jnp.float32)
    ext_knots = knots + 6
    ext_ids = jnp.arange(ext_knots, dtype=jnp.int32)
    band_weight = None
    for step in range(4):
        place = (ext_ids[None, :] == knot_ids[:, None] + 3 + step).astype(jnp.bfloat16)
        term = jnp.einsum("km,kab->kamb", place, blocks[:, step], preferred_element_type=jnp.bfloat16)
        band_weight = term if band_weight is None else band_weight + term
    for step in range(1, 4):
        place = (ext_ids[None, :] == knot_ids[:, None] + 3 - step).astype(jnp.bfloat16)
        band_weight = band_weight + jnp.einsum(
            "km,kba->kamb",
            place,
            lower_blocks[3 - step : 3 - step + knots, step],
            preferred_element_type=jnp.bfloat16,
        )
    fetch_order = [bucket_of[-s] for s in shifts]
    fetch_place = jnp.concatenate(
        [own_place.reshape(knots, buckets, slots)[:, b] for b in fetch_order], axis=1
    )
    fetch_blocks = jnp.concatenate([couplings[b] for b in fetch_order], axis=0)
    fetch_weight = jnp.einsum(
        "kf,fab->kafb", fetch_place.astype(jnp.bfloat16), fetch_blocks, preferred_element_type=jnp.bfloat16
    )
    weight = jnp.concatenate([band_weight, fetch_weight], axis=2)
    first_pick = jnp.stack([far_knot[bucket_of[-s]] for s in shifts])
    answer_pick = None
    land_place = None

    center = (HI_BOUND + LO_BOUND) / 2.0
    radius = (HI_BOUND - LO_BOUND) / 2.0
    coeff = radius / center
    solution = jnp.zeros(right_rows.shape, jnp.float32)
    residual = right_rows
    direction = right_rows / center
    own_rows = buckets * slots
    for turn in range(ITERS):
        probe_bf = direction.astype(jnp.bfloat16)
        solution = solution + direction
        if answer_pick is None:
            picked = jnp.einsum(
                "sk,kpr->spr", own_pick, probe_bf, preferred_element_type=jnp.float32
            ).astype(jnp.bfloat16)
            resident = picked.reshape(buckets, slots, params, probes)
        else:
            picked = jnp.einsum(
                "sk,kpr->spr",
                jnp.concatenate([own_pick, answer_pick], axis=0),
                probe_bf,
                preferred_element_type=jnp.float32,
            ).astype(jnp.bfloat16)
            resident = picked[:own_rows].reshape(buckets, slots, params, probes)
            answers = picked[own_rows:].reshape(len(shifts), slots, params, probes)
        product = jnp.einsum(
            "bsqp,bsqr->bspr", couplings, resident, preferred_element_type=jnp.float32
        ).astype(jnp.bfloat16)
        fetched = [None] * buckets
        landed = []
        received = []
        for t, s in enumerate(shifts):
            if answer_pick is None:
                message = jnp.concatenate(
                    [probe_bf, product[bucket_of[s]], index_rows[bucket_of[s]]], axis=0
                )
            else:
                message = jnp.concatenate([answers[t], product[bucket_of[s]]], axis=0)
            got = shifted_ring(message, "line", s)
            received.append(got)
            fetched[bucket_of[-s]] = got[:slots]
            landed.append(got[slots:])
        low = shifted_open(probe_bf[knots - 3 :], "seg", 1)
        high = shifted_open(probe_bf[:3], "seg", -1)
        if answer_pick is None:
            first_fetched, landed, heard = unpack_call(first_pick, received)
            heard = heard[:, :slots].astype(jnp.float32)
            answer_pick = jnp.concatenate(
                [(heard[shifts.index(-s)][:, None] == knot_vals[None, :]) for s in shifts], axis=0
            ).astype(jnp.bfloat16)
            land_place = (heard.reshape(-1)[None, :] == knot_vals[:, None]).astype(jnp.bfloat16)
        else:
            stacked = jnp.concatenate(
                [low, probe_bf, high] + [fetched[b] for b in fetch_order], axis=0
            )
            landed = jnp.concatenate(landed, axis=0)
        if turn == 0:
            extended = jnp.concatenate([low, probe_bf, high], axis=0)
            summed = jnp.einsum(
                "kamb,mbr->kar", band_weight, extended, preferred_element_type=jnp.float32
            ) + jnp.einsum(
                "kamb,mbr->kar", fetch_weight, first_fetched, preferred_element_type=jnp.float32
            )
        else:
            summed = jnp.einsum(
                "kamb,mbr->kar", weight, stacked, preferred_element_type=jnp.float32
            )
        cross = jnp.einsum("ks,spr->kpr", land_place, landed, preferred_element_type=jnp.float32)
        residual = residual - (summed + cross)
        coeff_next = 1.0 / (2.0 * center / radius - coeff)
        direction = coeff_next * coeff * direction + 2.0 * coeff_next / radius * residual
        coeff = coeff_next
    return (solution + direction)[None]


def solution(mesh):
    return jax.shard_map(
        body,
        mesh=mesh,
        in_specs=(
            P("line", "seg", None, None),
            P("line", "seg", None, None, None),
            P("line", "seg", None, None, None),
            P("line", "seg", None),
            P("line", "seg", None, None, None, None),
        ),
        out_specs=P("line", "seg", None, None),
        check_vma=False,
    )
```

```python
import jax
import jax.numpy as jnp
from jax import lax
from jax.sharding import PartitionSpec as P
from jax.experimental import pallas as pl
from jax.experimental.pallas import tpu as pltpu

ITERS = 3


LO_BOUND = 1.5
HI_BOUND = 12.0


def shifted_open(value, axis, steps):
    count = lax.axis_size(axis)
    initial, last = (max(0, -steps), min(count, count - steps))
    return lax.ppermute(value, axis, [(source, source + steps) for source in range(initial, last)])


def shifted_ring(value, axis, steps):
    count = lax.axis_size(axis)
    return lax.ppermute(value, axis, [(i, (i + steps) % count) for i in range(count)])


def unpack_first(pick_ref, *refs):
    messages = refs[:-3]
    fetched_ref, landed_ref, index_ref = refs[-3:]
    slots = pick_ref.shape[1]
    knots = messages[0].shape[0] - slots - 1
    for t, message in enumerate(messages):
        for slot in range(slots):
            knot = pick_ref[t, slot]
            row = message[jnp.minimum(jnp.maximum(knot, 0), knots - 1)]
            fetched_ref[t * slots + slot] = jnp.where(knot >= 0, row, jnp.zeros_like(row))
            landed_ref[t * slots + slot] = message[knots + slot]
        index_ref[t] = message[knots + slots, 0, :]


def unpack_call(pick, messages):
    rows, params, probes = messages[0].shape
    slots = pick.shape[1]
    count = len(messages)
    vmem = pl.BlockSpec(memory_space=pltpu.VMEM)
    return pl.pallas_call(
        unpack_first,
        out_shape=(
            jax.ShapeDtypeStruct((count * slots, params, probes), messages[0].dtype),
            jax.ShapeDtypeStruct((count * slots, params, probes), messages[0].dtype),
            jax.ShapeDtypeStruct((count, probes), messages[0].dtype),
        ),
        in_specs=[pl.BlockSpec(memory_space=pltpu.SMEM)] + [vmem] * count,
        out_specs=(vmem, vmem, vmem),
    )(pick, *messages)


def body(right_side, band_blocks, knot_pairs, pair_counts, cross_blocks):
    right_rows = right_side[0]
    blocks = band_blocks[0]
    my_pairs = knot_pairs[0, 0]
    used_count = pair_counts[0, 0]
    couplings = cross_blocks[0, 0]
    knots, params, probes = right_rows.shape
    buckets, slots = my_pairs.shape[0], my_pairs.shape[1]
    group_span = buckets // 2 + 1
    offsets = [
        b - (group_span - 1) if b < group_span - 1 else b - group_span + 2 for b in range(buckets)
    ]
    bucket_of = {o: b for b, o in enumerate(offsets)}
    shifts = [o for o in offsets if o > 0] + [o for o in offsets if o < 0]

    boundary_blocks = shifted_open(blocks[knots - 3 :], "seg", 1)
    lower_blocks = jnp.concatenate([boundary_blocks, blocks], axis=0)

    used = jnp.arange(slots, dtype=jnp.int32)[None, :] < used_count[:, None]
    own_knot = jnp.where(used, my_pairs[:, :, 0], -1)
    far_knot = jnp.where(used, my_pairs[:, :, 1], -1)
    knot_ids = jnp.arange(knots, dtype=jnp.int32)
    own_pick = (own_knot.reshape(-1)[:, None] == knot_ids[None, :]).astype(jnp.bfloat16)
    own_place = (own_knot.reshape(-1)[None, :] == knot_ids[:, None]).astype(jnp.float32)
    far_pick = (far_knot[:, :, None] == knot_ids[None, None, :]).astype(jnp.bfloat16)
    index_rows = jnp.zeros((buckets, 1, params, probes), jnp.bfloat16)
    index_rows = index_rows.at[:, 0, 0, :slots].set(far_knot.astype(jnp.bfloat16))
    knot_vals = knot_ids.astype(jnp.float32)
    ext_knots = knots + 6
    ext_ids = jnp.arange(ext_knots, dtype=jnp.int32)
    band_weight = None
    for step in range(4):
        place = (ext_ids[None, :] == knot_ids[:, None] + 3 + step).astype(jnp.bfloat16)
        term = jnp.einsum("km,kab->kamb", place, blocks[:, step], preferred_element_type=jnp.bfloat16)
        band_weight = term if band_weight is None else band_weight + term
    for step in range(1, 4):
        place = (ext_ids[None, :] == knot_ids[:, None] + 3 - step).astype(jnp.bfloat16)
        band_weight = band_weight + jnp.einsum(
            "km,kba->kamb",
            place,
            lower_blocks[3 - step : 3 - step + knots, step],
            preferred_element_type=jnp.bfloat16,
        )
    fetch_order = [bucket_of[-s] for s in shifts]
    fetch_place = jnp.concatenate(
        [own_place.reshape(knots, buckets, slots)[:, b] for b in fetch_order], axis=1
    )
    fetch_blocks = jnp.concatenate([couplings[b] for b in fetch_order], axis=0)
    fetch_weight = jnp.einsum(
        "kf,fab->kafb", fetch_place.astype(jnp.bfloat16), fetch_blocks, preferred_element_type=jnp.bfloat16
    )
    first_pick = jnp.stack([far_knot[bucket_of[-s]] for s in shifts])
    answer_pick = None
    land_place = None

    center = (HI_BOUND + LO_BOUND) / 2.0
    radius = (HI_BOUND - LO_BOUND) / 2.0
    coeff = radius / center
    solution = jnp.zeros(right_rows.shape, jnp.float32)
    residual = right_rows
    direction = right_rows / center
    own_rows = buckets * slots
    for turn in range(ITERS):
        probe_bf = direction.astype(jnp.bfloat16)
        solution = solution + direction
        if answer_pick is None:
            picked = jnp.einsum(
                "sk,kpr->spr", own_pick, probe_bf, preferred_element_type=jnp.float32
            ).astype(jnp.bfloat16)
            resident = picked.reshape(buckets, slots, params, probes)
        else:
            picked = jnp.einsum(
                "sk,kpr->spr",
                jnp.concatenate([own_pick, answer_pick], axis=0),
                probe_bf,
                preferred_element_type=jnp.float32,
            ).astype(jnp.bfloat16)
            resident = picked[:own_rows].reshape(buckets, slots, params, probes)
            answers = picked[own_rows:].reshape(len(shifts), slots, params, probes)
        product = jnp.einsum(
            "bsqp,bsqr->bspr", couplings, resident, preferred_element_type=jnp.float32
        ).astype(jnp.bfloat16)
        fetched = [None] * buckets
        landed = []
        received = []
        for t, s in enumerate(shifts):
            if answer_pick is None:
                message = jnp.concatenate(
                    [probe_bf, product[bucket_of[s]], index_rows[bucket_of[s]]], axis=0
                )
            else:
                message = jnp.concatenate([answers[t], product[bucket_of[s]]], axis=0)
            got = shifted_ring(message, "line", s)
            received.append(got)
            fetched[bucket_of[-s]] = got[:slots]
            landed.append(got[slots:])
        low = shifted_open(probe_bf[knots - 3 :], "seg", 1)
        high = shifted_open(probe_bf[:3], "seg", -1)
        if answer_pick is None:
            first_fetched, landed, heard = unpack_call(first_pick, received)
            heard = heard[:, :slots].astype(jnp.float32)
            answer_pick = jnp.concatenate(
                [(heard[shifts.index(-s)][:, None] == knot_vals[None, :]) for s in shifts], axis=0
            ).astype(jnp.bfloat16)
            land_place = (heard.reshape(-1)[None, :] == knot_vals[:, None]).astype(jnp.bfloat16)
        else:
            landed = jnp.concatenate(landed, axis=0)
        if turn == 0:
            fetched_rows = first_fetched
        else:
            fetched_rows = jnp.concatenate([fetched[b] for b in fetch_order], axis=0)
        extended = jnp.concatenate([low, probe_bf, high], axis=0)
        summed = jnp.einsum(
            "kamb,mbr->kar", band_weight, extended, preferred_element_type=jnp.float32
        ) + jnp.einsum(
            "kamb,mbr->kar", fetch_weight, fetched_rows, preferred_element_type=jnp.float32
        )
        cross = jnp.einsum("ks,spr->kpr", land_place, landed, preferred_element_type=jnp.float32)
        residual = residual - (summed + cross)
        coeff_next = 1.0 / (2.0 * center / radius - coeff)
        direction = coeff_next * coeff * direction + 2.0 * coeff_next / radius * residual
        coeff = coeff_next
    return (solution + direction)[None]


def solution(mesh):
    return jax.shard_map(
        body,
        mesh=mesh,
        in_specs=(
            P("line", "seg", None, None),
            P("line", "seg", None, None, None),
            P("line", "seg", None, None, None),
            P("line", "seg", None),
            P("line", "seg", None, None, None, None),
        ),
        out_specs=P("line", "seg", None, None),
        check_vma=False,
    )
```

```python
import jax
import jax.numpy as jnp
from jax import lax
from jax.sharding import PartitionSpec as P
from jax.experimental import pallas as pl
from jax.experimental.pallas import tpu as pltpu

ITERS = 3


LO_BOUND = 1.5
HI_BOUND = 12.0


def shifted_open(value, axis, steps):
    count = lax.axis_size(axis)
    initial, last = (max(0, -steps), min(count, count - steps))
    return lax.ppermute(value, axis, [(source, source + steps) for source in range(initial, last)])


def shifted_ring(value, axis, steps):
    count = lax.axis_size(axis)
    return lax.ppermute(value, axis, [(i, (i + steps) % count) for i in range(count)])


def unpack_first(pick_ref, *refs):
    messages = refs[:-3]
    fetched_ref, landed_ref, index_ref = refs[-3:]
    slots = pick_ref.shape[1]
    knots = messages[0].shape[0] - slots - 1
    for t, message in enumerate(messages):
        for slot in range(slots):
            knot = pick_ref[t, slot]
            row = message[jnp.minimum(jnp.maximum(knot, 0), knots - 1)]
            fetched_ref[t * slots + slot] = jnp.where(knot >= 0, row, jnp.zeros_like(row))
            landed_ref[t * slots + slot] = message[knots + slot]
        index_ref[t] = message[knots + slots, 0, :]


def unpack_call(pick, messages):
    rows, params, probes = messages[0].shape
    slots = pick.shape[1]
    count = len(messages)
    vmem = pl.BlockSpec(memory_space=pltpu.VMEM)
    return pl.pallas_call(
        unpack_first,
        out_shape=(
            jax.ShapeDtypeStruct((count * slots, params, probes), messages[0].dtype),
            jax.ShapeDtypeStruct((count * slots, params, probes), messages[0].dtype),
            jax.ShapeDtypeStruct((count, probes), messages[0].dtype),
        ),
        in_specs=[pl.BlockSpec(memory_space=pltpu.SMEM)] + [vmem] * count,
        out_specs=(vmem, vmem, vmem),
    )(pick, *messages)


def body(right_side, band_blocks, knot_pairs, pair_counts, cross_blocks):
    right_rows = right_side[0]
    blocks = band_blocks[0]
    my_pairs = knot_pairs[0, 0]
    used_count = pair_counts[0, 0]
    couplings = cross_blocks[0, 0]
    knots, params, probes = right_rows.shape
    buckets, slots = my_pairs.shape[0], my_pairs.shape[1]
    group_span = buckets // 2 + 1
    offsets = [
        b - (group_span - 1) if b < group_span - 1 else b - group_span + 2 for b in range(buckets)
    ]
    bucket_of = {o: b for b, o in enumerate(offsets)}
    shifts = [o for o in offsets if o > 0] + [o for o in offsets if o < 0]

    boundary_blocks = shifted_open(blocks[knots - 3 :], "seg", 1)
    lower_blocks = jnp.concatenate([boundary_blocks, blocks], axis=0)

    used = jnp.arange(slots, dtype=jnp.int32)[None, :] < used_count[:, None]
    own_knot = jnp.where(used, my_pairs[:, :, 0], -1)
    far_knot = jnp.where(used, my_pairs[:, :, 1], -1)
    knot_ids = jnp.arange(knots, dtype=jnp.int32)
    own_pick = (own_knot.reshape(-1)[:, None] == knot_ids[None, :]).astype(jnp.bfloat16)
    own_place = (own_knot.reshape(-1)[None, :] == knot_ids[:, None]).astype(jnp.float32)
    far_pick = (far_knot[:, :, None] == knot_ids[None, None, :]).astype(jnp.bfloat16)
    index_rows = jnp.zeros((buckets, 1, params, probes), jnp.bfloat16)
    index_rows = index_rows.at[:, 0, 0, :slots].set(far_knot.astype(jnp.bfloat16))
    knot_vals = knot_ids.astype(jnp.float32)
    ext_knots = knots + 6
    ext_ids = jnp.arange(ext_knots, dtype=jnp.int32)
    band_weight = None
    for step in range(4):
        place = (ext_ids[None, :] == knot_ids[:, None] + 3 + step).astype(jnp.bfloat16)
        term = jnp.einsum("km,kab->kamb", place, blocks[:, step], preferred_element_type=jnp.bfloat16)
        band_weight = term if band_weight is None else band_weight + term
    for step in range(1, 4):
        place = (ext_ids[None, :] == knot_ids[:, None] + 3 - step).astype(jnp.bfloat16)
        band_weight = band_weight + jnp.einsum(
            "km,kba->kamb",
            place,
            lower_blocks[3 - step : 3 - step + knots, step],
            preferred_element_type=jnp.bfloat16,
        )
    fetch_order = [bucket_of[-s] for s in shifts]
    fetch_place = jnp.concatenate(
        [own_place.reshape(knots, buckets, slots)[:, b] for b in fetch_order], axis=1
    )
    fetch_blocks = jnp.concatenate([couplings[b] for b in fetch_order], axis=0)
    fetch_weight = jnp.einsum(
        "kf,fab->kafb", fetch_place.astype(jnp.bfloat16), fetch_blocks, preferred_element_type=jnp.bfloat16
    )
    weight = jnp.concatenate([band_weight, fetch_weight], axis=2)
    first_pick = jnp.stack([far_knot[bucket_of[-s]] for s in shifts])
    answer_pick = None
    land_place = None

    center = (HI_BOUND + LO_BOUND) / 2.0
    radius = (HI_BOUND - LO_BOUND) / 2.0
    coeff = radius / center
    solution = jnp.zeros(right_rows.shape, jnp.float32)
    residual = right_rows
    direction = right_rows / center
    own_rows = buckets * slots
    for turn in range(ITERS):
        probe_bf = direction.astype(jnp.bfloat16)
        solution = solution + direction
        if answer_pick is None:
            picked = jnp.einsum(
                "sk,kpr->spr", own_pick, probe_bf, preferred_element_type=jnp.float32
            ).astype(jnp.bfloat16)
            resident = picked.reshape(buckets, slots, params, probes)
        else:
            picked = jnp.einsum(
                "sk,kpr->spr",
                jnp.concatenate([own_pick, answer_pick], axis=0),
                probe_bf,
                preferred_element_type=jnp.float32,
            ).astype(jnp.bfloat16)
            resident = picked[:own_rows].reshape(buckets, slots, params, probes)
            answers = picked[own_rows:].reshape(len(shifts), slots, params, probes)
        product = jnp.einsum(
            "bsqp,bsqr->bspr", couplings, resident, preferred_element_type=jnp.float32
        ).astype(jnp.bfloat16)
        fetched = [None] * buckets
        landed = []
        received = []
        for t, s in enumerate(shifts):
            if answer_pick is None:
                message = jnp.concatenate(
                    [probe_bf, product[bucket_of[s]], index_rows[bucket_of[s]]], axis=0
                )
            else:
                message = jnp.concatenate([answers[t], product[bucket_of[s]]], axis=0)
            got = shifted_ring(message, "line", s)
            received.append(got)
            fetched[bucket_of[-s]] = got[:slots]
            landed.append(got[slots:])
        tail_rows, head_rows = probe_bf[knots - 3 :], probe_bf[:3]
        if turn > 0:
            tail_rows, head_rows, _ = lax.optimization_barrier((tail_rows, head_rows, received[0]))
        low = shifted_open(tail_rows, "seg", 1)
        high = shifted_open(head_rows, "seg", -1)
        if answer_pick is None:
            first_fetched, landed, heard = unpack_call(first_pick, received)
            heard = heard[:, :slots].astype(jnp.float32)
            answer_pick = jnp.concatenate(
                [(heard[shifts.index(-s)][:, None] == knot_vals[None, :]) for s in shifts], axis=0
            ).astype(jnp.bfloat16)
            land_place = (heard.reshape(-1)[None, :] == knot_vals[:, None]).astype(jnp.bfloat16)
        else:
            stacked = jnp.concatenate(
                [low, probe_bf, high] + [fetched[b] for b in fetch_order], axis=0
            )
            landed = jnp.concatenate(landed, axis=0)
        if turn == 0:
            extended = jnp.concatenate([low, probe_bf, high], axis=0)
            summed = jnp.einsum(
                "kamb,mbr->kar", band_weight, extended, preferred_element_type=jnp.float32
            ) + jnp.einsum(
                "kamb,mbr->kar", fetch_weight, first_fetched, preferred_element_type=jnp.float32
            )
        else:
            summed = jnp.einsum(
                "kamb,mbr->kar", weight, stacked, preferred_element_type=jnp.float32
            )
        cross = jnp.einsum("ks,spr->kpr", land_place, landed, preferred_element_type=jnp.float32)
        residual = residual - (summed + cross)
        coeff_next = 1.0 / (2.0 * center / radius - coeff)
        direction = coeff_next * coeff * direction + 2.0 * coeff_next / radius * residual
        coeff = coeff_next
    return (solution + direction)[None]


def solution(mesh):
    return jax.shard_map(
        body,
        mesh=mesh,
        in_specs=(
            P("line", "seg", None, None),
            P("line", "seg", None, None, None),
            P("line", "seg", None, None, None),
            P("line", "seg", None),
            P("line", "seg", None, None, None, None),
        ),
        out_specs=P("line", "seg", None, None),
        check_vma=False,
    )
```

```python
import jax
import jax.numpy as jnp
from jax import lax
from jax.sharding import PartitionSpec as P
from jax.experimental import pallas as pl
from jax.experimental.pallas import tpu as pltpu

ITERS = 3


LO_BOUND = 1.5
HI_BOUND = 12.0


def shifted_open(value, axis, steps):
    count = lax.axis_size(axis)
    initial, last = (max(0, -steps), min(count, count - steps))
    return lax.ppermute(value, axis, [(source, source + steps) for source in range(initial, last)])


def shifted_ring(value, axis, steps):
    count = lax.axis_size(axis)
    return lax.ppermute(value, axis, [(i, (i + steps) % count) for i in range(count)])


def unpack_first(pick_ref, *refs):
    messages = refs[:-3]
    fetched_ref, landed_ref, index_ref = refs[-3:]
    slots = pick_ref.shape[1]
    knots = messages[0].shape[0] - slots - 1
    for t, message in enumerate(messages):
        for slot in range(slots):
            knot = pick_ref[t, slot]
            row = message[jnp.minimum(jnp.maximum(knot, 0), knots - 1)]
            fetched_ref[t * slots + slot] = jnp.where(knot >= 0, row, jnp.zeros_like(row))
            landed_ref[t * slots + slot] = message[knots + slot]
        index_ref[t] = message[knots + slots, 0, :]


def unpack_call(pick, messages):
    rows, params, probes = messages[0].shape
    slots = pick.shape[1]
    count = len(messages)
    vmem = pl.BlockSpec(memory_space=pltpu.VMEM)
    return pl.pallas_call(
        unpack_first,
        out_shape=(
            jax.ShapeDtypeStruct((count * slots, params, probes), messages[0].dtype),
            jax.ShapeDtypeStruct((count * slots, params, probes), messages[0].dtype),
            jax.ShapeDtypeStruct((count, probes), messages[0].dtype),
        ),
        in_specs=[pl.BlockSpec(memory_space=pltpu.SMEM)] + [vmem] * count,
        out_specs=(vmem, vmem, vmem),
    )(pick, *messages)


def body(right_side, band_blocks, knot_pairs, pair_counts, cross_blocks):
    right_rows = right_side[0]
    blocks = band_blocks[0]
    my_pairs = knot_pairs[0, 0]
    used_count = pair_counts[0, 0]
    couplings = cross_blocks[0, 0]
    knots, params, probes = right_rows.shape
    buckets, slots = my_pairs.shape[0], my_pairs.shape[1]
    group_span = buckets // 2 + 1
    offsets = [
        b - (group_span - 1) if b < group_span - 1 else b - group_span + 2 for b in range(buckets)
    ]
    bucket_of = {o: b for b, o in enumerate(offsets)}
    shifts = [o for o in offsets if o > 0] + [o for o in offsets if o < 0]

    boundary_blocks = shifted_open(blocks[knots - 3 :], "seg", 1)
    lower_blocks = jnp.concatenate([boundary_blocks, blocks], axis=0)

    used = jnp.arange(slots, dtype=jnp.int32)[None, :] < used_count[:, None]
    own_knot = jnp.where(used, my_pairs[:, :, 0], -1)
    far_knot = jnp.where(used, my_pairs[:, :, 1], -1)
    knot_ids = jnp.arange(knots, dtype=jnp.int32)
    own_pick = (own_knot.reshape(-1)[:, None] == knot_ids[None, :]).astype(jnp.bfloat16)
    own_place = (own_knot.reshape(-1)[None, :] == knot_ids[:, None]).astype(jnp.float32)
    far_pick = (far_knot[:, :, None] == knot_ids[None, None, :]).astype(jnp.bfloat16)
    index_rows = jnp.zeros((buckets, 1, params, probes), jnp.bfloat16)
    index_rows = index_rows.at[:, 0, 0, :slots].set(far_knot.astype(jnp.bfloat16))
    knot_vals = knot_ids.astype(jnp.float32)
    ext_knots = knots + 6
    ext_ids = jnp.arange(ext_knots, dtype=jnp.int32)
    band_weight = None
    for step in range(4):
        place = (ext_ids[None, :] == knot_ids[:, None] + 3 + step).astype(jnp.bfloat16)
        term = jnp.einsum("km,kab->kamb", place, blocks[:, step], preferred_element_type=jnp.bfloat16)
        band_weight = term if band_weight is None else band_weight + term
    for step in range(1, 4):
        place = (ext_ids[None, :] == knot_ids[:, None] + 3 - step).astype(jnp.bfloat16)
        band_weight = band_weight + jnp.einsum(
            "km,kba->kamb",
            place,
            lower_blocks[3 - step : 3 - step + knots, step],
            preferred_element_type=jnp.bfloat16,
        )
    fetch_order = [bucket_of[-s] for s in shifts]
    fetch_place = jnp.concatenate(
        [own_place.reshape(knots, buckets, slots)[:, b] for b in fetch_order], axis=1
    )
    fetch_blocks = jnp.concatenate([couplings[b] for b in fetch_order], axis=0)
    fetch_weight = jnp.einsum(
        "kf,fab->kafb", fetch_place.astype(jnp.bfloat16), fetch_blocks, preferred_element_type=jnp.bfloat16
    )
    weight = jnp.concatenate([band_weight, fetch_weight], axis=2)
    first_pick = jnp.stack([far_knot[bucket_of[-s]] for s in shifts])
    weight, band_weight, fetch_weight, direction_seed = lax.optimization_barrier(
        (weight, band_weight, fetch_weight, right_rows)
    )
    answer_pick = None
    land_place = None

    center = (HI_BOUND + LO_BOUND) / 2.0
    radius = (HI_BOUND - LO_BOUND) / 2.0
    coeff = radius / center
    solution = jnp.zeros(right_rows.shape, jnp.float32)
    residual = right_rows
    direction = direction_seed / center
    own_rows = buckets * slots
    for turn in range(ITERS):
        probe_bf = direction.astype(jnp.bfloat16)
        solution = solution + direction
        if answer_pick is None:
            picked = jnp.einsum(
                "sk,kpr->spr", own_pick, probe_bf, preferred_element_type=jnp.float32
            ).astype(jnp.bfloat16)
            resident = picked.reshape(buckets, slots, params, probes)
        else:
            picked = jnp.einsum(
                "sk,kpr->spr",
                jnp.concatenate([own_pick, answer_pick], axis=0),
                probe_bf,
                preferred_element_type=jnp.float32,
            ).astype(jnp.bfloat16)
            resident = picked[:own_rows].reshape(buckets, slots, params, probes)
            answers = picked[own_rows:].reshape(len(shifts), slots, params, probes)
        product = jnp.einsum(
            "bsqp,bsqr->bspr", couplings, resident, preferred_element_type=jnp.float32
        ).astype(jnp.bfloat16)
        fetched = [None] * buckets
        landed = []
        received = []
        for t, s in enumerate(shifts):
            if answer_pick is None:
                message = jnp.concatenate(
                    [probe_bf, product[bucket_of[s]], index_rows[bucket_of[s]]], axis=0
                )
            else:
                message = jnp.concatenate([answers[t], product[bucket_of[s]]], axis=0)
            got = shifted_ring(message, "line", s)
            received.append(got)
            fetched[bucket_of[-s]] = got[:slots]
            landed.append(got[slots:])
        low = shifted_open(probe_bf[knots - 3 :], "seg", 1)
        high = shifted_open(probe_bf[:3], "seg", -1)
        if answer_pick is None:
            first_fetched, landed, heard = unpack_call(first_pick, received)
            heard = heard[:, :slots].astype(jnp.float32)
            answer_pick = jnp.concatenate(
                [(heard[shifts.index(-s)][:, None] == knot_vals[None, :]) for s in shifts], axis=0
            ).astype(jnp.bfloat16)
            land_place = (heard.reshape(-1)[None, :] == knot_vals[:, None]).astype(jnp.bfloat16)
        else:
            stacked = jnp.concatenate(
                [low, probe_bf, high] + [fetched[b] for b in fetch_order], axis=0
            )
            landed = jnp.concatenate(landed, axis=0)
        if turn == 0:
            extended = jnp.concatenate([low, probe_bf, high], axis=0)
            summed = jnp.einsum(
                "kamb,mbr->kar", band_weight, extended, preferred_element_type=jnp.float32
            ) + jnp.einsum(
                "kamb,mbr->kar", fetch_weight, first_fetched, preferred_element_type=jnp.float32
            )
        else:
            summed = jnp.einsum(
                "kamb,mbr->kar", weight, stacked, preferred_element_type=jnp.float32
            )
        cross = jnp.einsum("ks,spr->kpr", land_place, landed, preferred_element_type=jnp.float32)
        residual = residual - (summed + cross)
        coeff_next = 1.0 / (2.0 * center / radius - coeff)
        direction = coeff_next * coeff * direction + 2.0 * coeff_next / radius * residual
        coeff = coeff_next
    return (solution + direction)[None]


def solution(mesh):
    return jax.shard_map(
        body,
        mesh=mesh,
        in_specs=(
            P("line", "seg", None, None),
            P("line", "seg", None, None, None),
            P("line", "seg", None, None, None),
            P("line", "seg", None),
            P("line", "seg", None, None, None, None),
        ),
        out_specs=P("line", "seg", None, None),
        check_vma=False,
    )
```

```python
import jax
import jax.numpy as jnp
from jax import lax
from jax.sharding import PartitionSpec as P
from jax.experimental import pallas as pl
from jax.experimental.pallas import tpu as pltpu

ITERS = 3


LO_BOUND = 1.5
HI_BOUND = 12.0


def shifted_open(value, axis, steps):
    count = lax.axis_size(axis)
    initial, last = (max(0, -steps), min(count, count - steps))
    return lax.ppermute(value, axis, [(source, source + steps) for source in range(initial, last)])


def shifted_ring(value, axis, steps):
    count = lax.axis_size(axis)
    return lax.ppermute(value, axis, [(i, (i + steps) % count) for i in range(count)])


def unpack_first(pick_ref, *refs):
    messages = refs[:-3]
    fetched_ref, landed_ref, index_ref = refs[-3:]
    slots = pick_ref.shape[1]
    knots = messages[0].shape[0] - slots - 1
    for t, message in enumerate(messages):
        for slot in range(slots):
            knot = pick_ref[t, slot]
            row = message[jnp.minimum(jnp.maximum(knot, 0), knots - 1)]
            fetched_ref[t * slots + slot] = jnp.where(knot >= 0, row, jnp.zeros_like(row))
            landed_ref[t * slots + slot] = message[knots + slot]
        index_ref[t] = message[knots + slots, 0, :]


def unpack_call(pick, messages):
    rows, params, probes = messages[0].shape
    slots = pick.shape[1]
    count = len(messages)
    vmem = pl.BlockSpec(memory_space=pltpu.VMEM)
    return pl.pallas_call(
        unpack_first,
        out_shape=(
            jax.ShapeDtypeStruct((count * slots, params, probes), messages[0].dtype),
            jax.ShapeDtypeStruct((count * slots, params, probes), messages[0].dtype),
            jax.ShapeDtypeStruct((count, probes), messages[0].dtype),
        ),
        in_specs=[pl.BlockSpec(memory_space=pltpu.SMEM)] + [vmem] * count,
        out_specs=(vmem, vmem, vmem),
    )(pick, *messages)


def body(right_side, band_blocks, knot_pairs, pair_counts, cross_blocks):
    right_rows = right_side[0]
    blocks = band_blocks[0]
    my_pairs = knot_pairs[0, 0]
    used_count = pair_counts[0, 0]
    couplings = cross_blocks[0, 0]
    knots, params, probes = right_rows.shape
    buckets, slots = my_pairs.shape[0], my_pairs.shape[1]
    group_span = buckets // 2 + 1
    offsets = [
        b - (group_span - 1) if b < group_span - 1 else b - group_span + 2 for b in range(buckets)
    ]
    bucket_of = {o: b for b, o in enumerate(offsets)}
    shifts = [o for o in offsets if o > 0] + [o for o in offsets if o < 0][::-1]

    boundary_blocks = shifted_open(blocks[knots - 3 :], "seg", 1)
    lower_blocks = jnp.concatenate([boundary_blocks, blocks], axis=0)

    used = jnp.arange(slots, dtype=jnp.int32)[None, :] < used_count[:, None]
    own_knot = jnp.where(used, my_pairs[:, :, 0], -1)
    far_knot = jnp.where(used, my_pairs[:, :, 1], -1)
    knot_ids = jnp.arange(knots, dtype=jnp.int32)
    own_pick = (own_knot.reshape(-1)[:, None] == knot_ids[None, :]).astype(jnp.bfloat16)
    own_place = (own_knot.reshape(-1)[None, :] == knot_ids[:, None]).astype(jnp.float32)
    far_pick = (far_knot[:, :, None] == knot_ids[None, None, :]).astype(jnp.bfloat16)
    index_rows = jnp.zeros((buckets, 1, params, probes), jnp.bfloat16)
    index_rows = index_rows.at[:, 0, 0, :slots].set(far_knot.astype(jnp.bfloat16))
    knot_vals = knot_ids.astype(jnp.float32)
    ext_knots = knots + 6
    ext_ids = jnp.arange(ext_knots, dtype=jnp.int32)
    band_weight = None
    for step in range(4):
        place = (ext_ids[None, :] == knot_ids[:, None] + 3 + step).astype(jnp.bfloat16)
        term = jnp.einsum("km,kab->kamb", place, blocks[:, step], preferred_element_type=jnp.bfloat16)
        band_weight = term if band_weight is None else band_weight + term
    for step in range(1, 4):
        place = (ext_ids[None, :] == knot_ids[:, None] + 3 - step).astype(jnp.bfloat16)
        band_weight = band_weight + jnp.einsum(
            "km,kba->kamb",
            place,
            lower_blocks[3 - step : 3 - step + knots, step],
            preferred_element_type=jnp.bfloat16,
        )
    fetch_order = [bucket_of[-s] for s in shifts]
    fetch_place = jnp.concatenate(
        [own_place.reshape(knots, buckets, slots)[:, b] for b in fetch_order], axis=1
    )
    fetch_blocks = jnp.concatenate([couplings[b] for b in fetch_order], axis=0)
    fetch_weight = jnp.einsum(
        "kf,fab->kafb", fetch_place.astype(jnp.bfloat16), fetch_blocks, preferred_element_type=jnp.bfloat16
    )
    weight = jnp.concatenate([band_weight, fetch_weight], axis=2)
    first_pick = jnp.stack([far_knot[bucket_of[-s]] for s in shifts])
    answer_pick = None
    land_place = None

    center = (HI_BOUND + LO_BOUND) / 2.0
    radius = (HI_BOUND - LO_BOUND) / 2.0
    coeff = radius / center
    solution = jnp.zeros(right_rows.shape, jnp.float32)
    residual = right_rows
    direction = right_rows / center
    own_rows = buckets * slots
    for turn in range(ITERS):
        probe_bf = direction.astype(jnp.bfloat16)
        solution = solution + direction
        if answer_pick is None:
            picked = jnp.einsum(
                "sk,kpr->spr", own_pick, probe_bf, preferred_element_type=jnp.float32
            ).astype(jnp.bfloat16)
            resident = picked.reshape(buckets, slots, params, probes)
        else:
            picked = jnp.einsum(
                "sk,kpr->spr",
                jnp.concatenate([own_pick, answer_pick], axis=0),
                probe_bf,
                preferred_element_type=jnp.float32,
            ).astype(jnp.bfloat16)
            resident = picked[:own_rows].reshape(buckets, slots, params, probes)
            answers = picked[own_rows:].reshape(len(shifts), slots, params, probes)
        product = jnp.einsum(
            "bsqp,bsqr->bspr", couplings, resident, preferred_element_type=jnp.float32
        ).astype(jnp.bfloat16)
        fetched = [None] * buckets
        landed = []
        received = []
        for t, s in enumerate(shifts):
            if answer_pick is None:
                message = jnp.concatenate(
                    [probe_bf, product[bucket_of[s]], index_rows[bucket_of[s]]], axis=0
                )
            else:
                message = jnp.concatenate([answers[t], product[bucket_of[s]]], axis=0)
            got = shifted_ring(message, "line", s)
            received.append(got)
            fetched[bucket_of[-s]] = got[:slots]
            landed.append(got[slots:])
        low = shifted_open(probe_bf[knots - 3 :], "seg", 1)
        high = shifted_open(probe_bf[:3], "seg", -1)
        if answer_pick is None:
            first_fetched, landed, heard = unpack_call(first_pick, received)
            heard = heard[:, :slots].astype(jnp.float32)
            answer_pick = jnp.concatenate(
                [(heard[shifts.index(-s)][:, None] == knot_vals[None, :]) for s in shifts], axis=0
            ).astype(jnp.bfloat16)
            land_place = (heard.reshape(-1)[None, :] == knot_vals[:, None]).astype(jnp.bfloat16)
        else:
            stacked = jnp.concatenate(
                [low, probe_bf, high] + [fetched[b] for b in fetch_order], axis=0
            )
            landed = jnp.concatenate(landed, axis=0)
        if turn == 0:
            extended = jnp.concatenate([low, probe_bf, high], axis=0)
            summed = jnp.einsum(
                "kamb,mbr->kar", band_weight, extended, preferred_element_type=jnp.float32
            ) + jnp.einsum(
                "kamb,mbr->kar", fetch_weight, first_fetched, preferred_element_type=jnp.float32
            )
        else:
            summed = jnp.einsum(
                "kamb,mbr->kar", weight, stacked, preferred_element_type=jnp.float32
            )
        cross = jnp.einsum("ks,spr->kpr", land_place, landed, preferred_element_type=jnp.float32)
        residual = residual - (summed + cross)
        coeff_next = 1.0 / (2.0 * center / radius - coeff)
        direction = coeff_next * coeff * direction + 2.0 * coeff_next / radius * residual
        coeff = coeff_next
    return (solution + direction)[None]


def solution(mesh):
    return jax.shard_map(
        body,
        mesh=mesh,
        in_specs=(
            P("line", "seg", None, None),
            P("line", "seg", None, None, None),
            P("line", "seg", None, None, None),
            P("line", "seg", None),
            P("line", "seg", None, None, None, None),
        ),
        out_specs=P("line", "seg", None, None),
        check_vma=False,
    )
```
